128 devices in a mesh: view: 4 (over y), gauss: 32 (over z, x, core).
Axes of the slice: x: 4, y: 4, z: 4, core: 2. Of those that a mesh axis runs over, the one named last changes fastest.
Arguments:
- jac: bfloat16 [4, 128, 59, 128, 256], P('view', 'gauss'), may hold values from -0.375 to 0.375
- tile_count: int32 [4, 32], P('view', 'gauss'), may hold values from 1 to 4, as said below
- tile_block: int32 [4, 128], P('view', 'gauss'), may hold values from 0 to 1
- tile_pix: int32 [4, 128], P('view', 'gauss'), may hold values from 0 to 4095
- residual: bfloat16 [4, 4096, 256], P('view'), may hold values from -6 to 6
- direction: bfloat16 [64, 59, 128], P('gauss'), may hold values from -0.75 to 0.75
Outputs:
- gradient: float32 [64, 59, 128], P('gauss')
- curvature: float32 [64, 59, 128], P('gauss')
- precond: float32 [64, 59, 59, 128], P('gauss')
The draws below stay inside these ranges and needn't reach their ends.
Inputs may be any that keep to these rules, and one draw needn't show every extreme that they name: `tile_count`: every device has at least one live tile, and some device has all 4 slots live.
All inputs are finite; a program needn't handle non-finite values.
Results may differ from the reference program's by a relative error of at most 0.0028.
Values sent between devices are 32-bit elements; how exact they have to be, the bound alone decides.
No kernel may reach another device: no remote copies, remote signals or barrier semaphores. Data moves between devices by JAX's collectives and lax.ppermute only.
A program may use at most 128 MiB of HBM per device.

```python
import math
import jax
import jax.numpy as jnp
import numpy as np
from jax import lax

P_SIZE = 59
GB = 128
PIX = 256
T_SLOT = 4
B_Q = 2
PBV = 4096
SLABS = 4
OWNERS = 32
TILES = 128
NB = 64


def draw_tile_count(key, part):
    counts = jax.random.randint(key, (SLABS, OWNERS), 1, T_SLOT + 1)
    return counts.at[0, 0].set(T_SLOT).astype(jnp.int32)


def touch_ends(result, own_key, low, largest):
    longest = result.shape.index(max(result.shape))
    spots = []
    for shift in (0, 1):
        where = [jax.random.randint(jax.random.fold_in(own_key, axis), (), 0, length) for axis, length in enumerate(result.shape)]
        where[longest] = (where[longest] + shift) % result.shape[longest]
        spots.append(tuple(where))
    return result.at[spots[0]].set(low).at[spots[1]].set(largest)


def block_scale(own_key, extent, cuts, low, largest):
    factor_of, own = 1.0, jax.random.fold_in(own_key, 6)
    for dim, parts in cuts:
        steps = jnp.exp(jax.random.uniform(jax.random.fold_in(own, dim), (parts,), jnp.float32, low / len(cuts), largest / len(cuts)))
        factor_of = factor_of * jnp.repeat(steps, extent[dim] // parts).reshape([-1 if axis == dim else 1 for axis in range(len(extent))])
    return factor_of


def rank_bounds(number_of, slope):
    portions = [(1 << 20) // math.isqrt(grade ** slope) + 1 for grade in range(1, number_of + 1)]
    spread = 1 + sum(portions) // (1 << 30)
    return np.cumsum(np.array([max(1, weight // spread) for weight in portions]))


def ranked_ids(own_key, dims, number_of, lean):
    grid = rank_bounds(number_of, lean)
    pick = jax.random.randint(jax.random.fold_in(own_key, 1), dims, 0, int(grid[number_of - 1]))
    standing = jnp.searchsorted(jnp.asarray(grid, jnp.int32), pick, side="right")
    return jax.random.permutation(jax.random.fold_in(own_key, 2), number_of)[standing].astype(jnp.int32)


def bell_draw(stream_key, dims, deviation, reach, split=(), kind=jnp.bfloat16):
    values = jax.random.normal(stream_key, dims, jnp.float32) * deviation
    if len(split) > 0:
        values = block_scale(stream_key, dims, split, -0.22, 0.18) * values
    return jnp.clip(values, min=-reach, max=reach).astype(kind)


def setup_inputs(seed: int = 0) -> dict:
    keys = jax.random.split(jax.random.key(seed), 7)
    jac = bell_draw(keys[0], (SLABS, TILES, P_SIZE, GB, PIX), 0.0625, 0.375, ((0, 4), (1, 32)))
    tile_count = draw_tile_count(jax.random.fold_in(keys[6], 71), 0)
    tile_block = touch_ends(jax.random.randint(keys[2], (SLABS, TILES), 0, B_Q), jax.random.fold_in(keys[2], 1), 0, B_Q - 1).astype(jnp.int32)
    tile_pix = touch_ends(ranked_ids(keys[3], (SLABS, TILES), PBV, 2), jax.random.fold_in(keys[3], 3), 0, PBV - 1).astype(jnp.int32)
    residual = bell_draw(keys[4], (SLABS, PBV, PIX), 1.0, 6.0, ((0, 4),))
    direction = bell_draw(keys[5], (NB, P_SIZE, GB), 0.125, 0.75, ((0, 32),))
    return dict(jac=jac, tile_count=tile_count, tile_block=tile_block, tile_pix=tile_pix, residual=residual, direction=direction)


def reference(jac, tile_count, tile_block, tile_pix, residual, direction):
    slot_number = jnp.arange(TILES) % T_SLOT
    owner_number = jnp.arange(TILES) // T_SLOT
    alive_mask = (slot_number[None, :] < tile_count[:, owner_number]).astype(jnp.float32)
    global_block = owner_number[None, :] * B_Q + tile_block
    flat_jac = jac.reshape(SLABS * TILES, P_SIZE, GB, PIX)
    flat_block = global_block.reshape(-1).astype(jnp.int32)
    flat_pix = tile_pix.reshape(-1).astype(jnp.int32)
    flat_alive = alive_mask.reshape(-1)
    flat_slab = (jnp.arange(SLABS * TILES) // TILES).astype(jnp.int32)

    def shade_one(items):
        tile_now, block_id, alive_now = items
        weights = direction[block_id].astype(jnp.float32)
        shading = jnp.einsum('pgx,pg->x', tile_now.astype(jnp.float32), weights, precision=lax.Precision.HIGHEST)
        return shading * alive_now

    shade = lax.map(shade_one, (flat_jac, flat_block, flat_alive)).reshape(SLABS, TILES, PIX)
    one_hot = (tile_pix[:, :, None] == jnp.arange(PBV)[None, None, :]).astype(jnp.float32)
    pixel_jp = jnp.einsum('vtk,vtx->vkx', one_hot, shade, precision=lax.Precision.HIGHEST)
    jp_round = pixel_jp.astype(jnp.bfloat16)

    def accumulate(state_now, items):
        grad_acc, curv_acc, gram_acc = state_now
        tile_now, block_id, pix_id, slab_id, alive_now = items
        tile_wide = tile_now.astype(jnp.float32)
        resid_row = residual[slab_id, pix_id].astype(jnp.float32)
        jp_row = jp_round[slab_id, pix_id].astype(jnp.float32)
        grad_term = jnp.einsum('pgx,x->pg', tile_wide, resid_row, precision=lax.Precision.HIGHEST) * alive_now
        curv_term = jnp.einsum('pgx,x->pg', tile_wide, jp_row, precision=lax.Precision.HIGHEST) * alive_now
        gram_term = jnp.einsum('pgx,qgx->pqg', tile_wide, tile_wide, precision=lax.Precision.HIGHEST) * alive_now
        grad_acc = grad_acc.at[block_id].add(grad_term)
        curv_acc = curv_acc.at[block_id].add(curv_term)
        gram_acc = gram_acc.at[block_id].add(gram_term)
        return (grad_acc, curv_acc, gram_acc), None

    start = (jnp.zeros((NB, P_SIZE, GB), jnp.float32), jnp.zeros((NB, P_SIZE, GB), jnp.float32), jnp.zeros((NB, P_SIZE, P_SIZE, GB), jnp.float32))
    finals, unused = lax.scan(accumulate, start, (flat_jac, flat_block, flat_pix, flat_slab, flat_alive))
    return finals[0], finals[1], finals[2]
```

```python
import math

import jax
import jax.numpy as jnp
import numpy as np
from jax import lax
from jax.sharding import PartitionSpec as P


def side_by_side(arrays, axis, dim, along):
    widths = [math.prod(a.shape[along:]) for a in arrays]
    both = jnp.concatenate(
        [a.reshape(*a.shape[:along], w) for a, w in zip(arrays, widths)], axis=along
    )
    result = lax.all_gather(both, axis, axis=dim, tiled=True)
    blocks = jnp.split(result, [sum(widths[:k]) for k in range(1, len(widths))], axis=along)
    return tuple(
        (b.reshape(*result.shape[:along], *a.shape[along:]) for a, b in zip(arrays, blocks))
    )


def copy_for_each(array, axis):
    length = lax.axis_size(axis)
    return lax.all_to_all(
        jnp.broadcast_to(array[None], (length, *array.shape)), axis, 0, 0, tiled=True
    )


def over_copies(array, axis):
    everything = copy_for_each(array, axis)
    return jnp.sum(everything, axis=0)


def upper_index(size):
    p_id, q_id = np.triu_indices(size)
    return p_id.astype(np.int32), q_id.astype(np.int32)


def pack_upper(gram):
    p_id, q_id = upper_index(gram.shape[1])
    return gram[:, p_id, q_id, :]


def unpack_upper(packed, size):
    slot = np.zeros((size, size), np.int32)
    p_id, q_id = upper_index(size)
    slot[p_id, q_id] = np.arange(p_id.size)
    slot[q_id, p_id] = np.arange(p_id.size)
    return jnp.take(packed, jnp.asarray(slot), axis=1)


def local(jac, tile_count, tile_block, tile_pix, residual, direction):
    slot_total = jac.shape[1]
    blocks = direction.shape[0]
    size = jac.shape[2]
    live_count = tile_count[0, 0]
    block_ids = tile_block[0]
    pix_ids = tile_pix[0]
    alive_mask = jnp.arange(slot_total) < live_count
    alive_float = alive_mask.astype(jnp.float32)
    tiles_now = jac[0]
    block_match = block_ids[:, None] == jnp.arange(blocks)[None, :]
    block_hot = (block_match & alive_mask[:, None]).astype(jnp.float32)

    gram_terms = jnp.einsum(
        "tpgx,tqgx->tpqg", tiles_now, tiles_now, preferred_element_type=jnp.float32
    )
    gram_acc = jnp.sum(block_hot.T[:, :, None, None, None] * gram_terms[None], axis=1)
    resid_rows = jnp.take(residual[0], pix_ids, axis=0)
    grad_terms = jnp.einsum(
        "tpgx,tx->tpg", tiles_now, resid_rows, preferred_element_type=jnp.float32
    )
    grad_acc = jnp.sum(block_hot.T[:, :, None, None] * grad_terms[None], axis=1)
    payload = jnp.concatenate([pack_upper(gram_acc), grad_acc], axis=1)
    summed = lax.psum(payload, "view")
    packed_rows = size * (size + 1) // 2
    gram_sum = unpack_upper(summed[:, :packed_rows], size)
    grad_sum = summed[:, packed_rows:]

    dir_rows = jnp.take(direction, block_ids, axis=0)
    shade_rows = (
        jnp.einsum("tpgx,tpg->tx", tiles_now, dir_rows, preferred_element_type=jnp.float32)
        * alive_float[:, None]
    )
    tagged = jnp.where(alive_mask, pix_ids + 1, 0).astype(jnp.float32)
    all_rows, all_tags = side_by_side((shade_rows, tagged), "gauss", 0, 1)
    own_tags = jnp.where(alive_mask, pix_ids + 1, -1).astype(jnp.float32)
    match_hot = (own_tags[:, None] == all_tags[None, :]).astype(jnp.float32)
    jp_rows = jnp.dot(match_hot, all_rows, precision=lax.Precision.HIGHEST)
    jp_round = jp_rows.astype(jnp.bfloat16)
    curv_terms = jnp.einsum("tpgx,tx->tpg", tiles_now, jp_round, preferred_element_type=jnp.float32)
    curv_acc = jnp.sum(block_hot.T[:, :, None, None] * curv_terms[None], axis=1)
    curv_sum = over_copies(curv_acc, "view")
    return (grad_sum, curv_sum, gram_sum)


def solution(mesh):
    placed = (
        P("view", "gauss", None, None, None),
        P("view", "gauss"),
        P("view", "gauss"),
        P("view", "gauss"),
        P("view", None, None),
        P("gauss", None, None),
    )
    return jax.shard_map(
        local,
        mesh=mesh,
        in_specs=placed,
        out_specs=(P("gauss", None, None), P("gauss", None, None), P("gauss", None, None, None)),
        check_vma=False,
    )
```

```python
import math

import jax
import jax.numpy as jnp
import numpy as np
from jax import lax
from jax.sharding import PartitionSpec as P
from jax.experimental import pallas as pl
from jax.experimental.pallas import tpu as pltpu


def side_by_side(arrays, axis, dim, along):
    widths = [math.prod(a.shape[along:]) for a in arrays]
    both = jnp.concatenate(
        [a.reshape(*a.shape[:along], w) for a, w in zip(arrays, widths)], axis=along
    )
    result = lax.all_gather(both, axis, axis=dim, tiled=True)
    blocks = jnp.split(result, [sum(widths[:k]) for k in range(1, len(widths))], axis=along)
    return tuple(
        (b.reshape(*result.shape[:along], *a.shape[along:]) for a, b in zip(arrays, blocks))
    )


def copy_for_each(array, axis):
    length = lax.axis_size(axis)
    return lax.all_to_all(
        jnp.broadcast_to(array[None], (length, *array.shape)), axis, 0, 0, tiled=True
    )


def over_copies(array, axis):
    everything = copy_for_each(array, axis)
    return jnp.sum(everything, axis=0)


P_PAD = 64
GROUP = 4


def row_offsets(size):
    return [p * size - p * (p - 1) // 2 for p in range(size)]


def gram_kernel(w_ref, jac_ref, out_ref, xf_ref, sc_ref, acc_ref):
    t = pl.program_id(0)
    size = jac_ref.shape[0]
    gb = jac_ref.shape[1]
    nb = acc_ref.shape[0]

    @pl.when(t == 0)
    def _init():
        for h in range(xf_ref.shape[0]):
            xf_ref[h, pl.ds(size * gb, (P_PAD - size) * gb), :] = jnp.zeros(((P_PAD - size) * gb, 128), jnp.float32)
        acc_ref[...] = jnp.zeros(acc_ref.shape, jnp.float32)

    halves = xf_ref.shape[0]
    for p in range(size):
        for h in range(halves):
            xf_ref[h, pl.ds(p * gb, gb), :] = jac_ref[p, :, h * 128:(h + 1) * 128].astype(jnp.float32)

    for c in range(gb // GROUP):
        parts = [
            jnp.concatenate([xf_ref[h, pl.ds(c * GROUP + i, P_PAD, stride=gb), :] for h in range(halves)], axis=1)
            for i in range(GROUP)
        ]
        a = jnp.concatenate(parts, axis=0).astype(jnp.bfloat16)
        prod = lax.dot_general(a, a, (((1,), (1,)), ((), ())), preferred_element_type=jnp.float32)
        for i in range(GROUP):
            g = c * GROUP + i
            lane0 = 128 * ((i * P_PAD) // 128)
            sc_ref[pl.ds(g * P_PAD, P_PAD), :] = prod[i * P_PAD:(i + 1) * P_PAD, lane0:lane0 + 128]

    odd = (lax.broadcasted_iota(jnp.int32, (P_PAD, gb), 1) % 2) == 1
    weights = [w_ref[t, b] for b in range(nb)]
    for p in range(size):
        s = sc_ref[pl.ds(p, gb, stride=P_PAD), :]
        tr = s.T
        row = jnp.where(odd, tr[P_PAD:2 * P_PAD], tr[0:P_PAD])
        for b in range(nb):
            acc_ref[b, p] += weights[b] * row

    @pl.when(t == pl.num_programs(0) - 1)
    def _pack():
        offs = row_offsets(size)
        for b in range(nb):
            for p in range(size):
                out_ref[b, pl.ds(offs[p], size - p), :] = acc_ref[b, p, pl.ds(p, size - p), :]


def gram_packed(tiles, weights):
    nt, size, gb, nx = tiles.shape
    nb = weights.shape[1]
    packed_rows = size * (size + 1) // 2
    return pl.pallas_call(
        gram_kernel,
        grid=(nt,),
        in_specs=[
            pl.BlockSpec(memory_space=pltpu.SMEM),
            pl.BlockSpec((None, size, gb, nx), lambda t: (t, 0, 0, 0)),
        ],
        out_specs=pl.BlockSpec((nb, packed_rows, gb), lambda t: (0, 0, 0)),
        out_shape=jax.ShapeDtypeStruct((nb, packed_rows, gb), jnp.float32),
        scratch_shapes=[
            pltpu.VMEM((nx // 128, P_PAD * gb, 128), jnp.float32),
            pltpu.VMEM((gb * P_PAD, 128), jnp.float32),
            pltpu.VMEM((nb, size, P_PAD, gb), jnp.float32),
        ],
        compiler_params=pltpu.CompilerParams(vmem_limit_bytes=48 * 1024 * 1024),
    )(weights, tiles)


def unpack_kernel(packed_ref, out_ref, u_ref):
    nb, size = out_ref.shape[0], out_ref.shape[1]
    offs = row_offsets(size)
    q_id = lax.broadcasted_iota(jnp.int32, (P_PAD, out_ref.shape[3]), 0)
    for b in range(nb):
        for p in range(size):
            u_ref[pl.ds(p * P_PAD + p, size - p), :] = packed_ref[b, pl.ds(offs[p], size - p), :]
        for p in range(size):
            up = u_ref[pl.ds(p * P_PAD, P_PAD), :]
            low = u_ref[pl.ds(p, P_PAD, stride=P_PAD), :]
            full = jnp.where(q_id >= p, up, low)
            out_ref[b, p] = full[0:size]


def unpack(packed, size):
    nb, _, gb = packed.shape
    return pl.pallas_call(
        unpack_kernel,
        in_specs=[pl.BlockSpec(memory_space=pltpu.VMEM)],
        out_specs=pl.BlockSpec(memory_space=pltpu.VMEM),
        out_shape=jax.ShapeDtypeStruct((nb, size, size, gb), jnp.float32),
        scratch_shapes=[pltpu.VMEM((P_PAD * P_PAD, gb), jnp.float32)],
    )(packed)


def local(jac, tile_count, tile_block, tile_pix, residual, direction):
    slot_total = jac.shape[1]
    blocks = direction.shape[0]
    size = jac.shape[2]
    live_count = tile_count[0, 0]
    block_ids = tile_block[0]
    pix_ids = tile_pix[0]
    alive_mask = jnp.arange(slot_total) < live_count
    alive_float = alive_mask.astype(jnp.float32)
    tiles_now = jac[0]
    block_match = block_ids[:, None] == jnp.arange(blocks)[None, :]
    block_hot = (block_match & alive_mask[:, None]).astype(jnp.float32)

    packed_gram = gram_packed(tiles_now, block_hot)
    resid_rows = jnp.take(residual[0], pix_ids, axis=0)
    grad_terms = jnp.einsum(
        "tpgx,tx->tpg", tiles_now, resid_rows, preferred_element_type=jnp.float32
    )
    grad_acc = jnp.sum(block_hot.T[:, :, None, None] * grad_terms[None], axis=1)
    payload = jnp.concatenate([packed_gram, grad_acc], axis=1)
    summed = lax.psum(payload, "view")
    packed_rows = size * (size + 1) // 2
    gram_sum = unpack(summed[:, :packed_rows], size)
    grad_sum = summed[:, packed_rows:]

    dir_rows = jnp.take(direction, block_ids, axis=0)
    shade_rows = (
        jnp.einsum("tpgx,tpg->tx", tiles_now, dir_rows, preferred_element_type=jnp.float32)
        * alive_float[:, None]
    )
    tagged = jnp.where(alive_mask, pix_ids + 1, 0).astype(jnp.float32)
    all_rows, all_tags = side_by_side((shade_rows, tagged), "gauss", 0, 1)
    own_tags = jnp.where(alive_mask, pix_ids + 1, -1).astype(jnp.float32)
    match_hot = (own_tags[:, None] == all_tags[None, :]).astype(jnp.float32)
    jp_rows = jnp.dot(match_hot, all_rows, precision=lax.Precision.HIGHEST)
    jp_round = jp_rows.astype(jnp.bfloat16)
    curv_terms = jnp.einsum("tpgx,tx->tpg", tiles_now, jp_round, preferred_element_type=jnp.float32)
    curv_acc = jnp.sum(block_hot.T[:, :, None, None] * curv_terms[None], axis=1)
    curv_sum = over_copies(curv_acc, "view")
    return (grad_sum, curv_sum, gram_sum)


def solution(mesh):
    placed = (
        P("view", "gauss", None, None, None),
        P("view", "gauss"),
        P("view", "gauss"),
        P("view", "gauss"),
        P("view", None, None),
        P("gauss", None, None),
    )
    return jax.shard_map(
        local,
        mesh=mesh,
        in_specs=placed,
        out_specs=(P("gauss", None, None), P("gauss", None, None), P("gauss", None, None, None)),
        check_vma=False,
    )
```

```python
import math

import jax
import jax.numpy as jnp
import numpy as np
from jax import lax
from jax.sharding import PartitionSpec as P
from jax.experimental import pallas as pl
from jax.experimental.pallas import tpu as pltpu


def side_by_side(arrays, axis, dim, along):
    widths = [math.prod(a.shape[along:]) for a in arrays]
    both = jnp.concatenate(
        [a.reshape(*a.shape[:along], w) for a, w in zip(arrays, widths)], axis=along
    )
    result = lax.all_gather(both, axis, axis=dim, tiled=True)
    blocks = jnp.split(result, [sum(widths[:k]) for k in range(1, len(widths))], axis=along)
    return tuple(
        (b.reshape(*result.shape[:along], *a.shape[along:]) for a, b in zip(arrays, blocks))
    )


def copy_for_each(array, axis):
    length = lax.axis_size(axis)
    return lax.all_to_all(
        jnp.broadcast_to(array[None], (length, *array.shape)), axis, 0, 0, tiled=True
    )


def over_copies(array, axis):
    everything = copy_for_each(array, axis)
    return jnp.sum(everything, axis=0)


P_PAD = 64
GROUP = 4


def row_offsets(size):
    return [p * size - p * (p - 1) // 2 for p in range(size)]


def gram_kernel(w_ref, jac_ref, out_ref, xf_ref, sc_ref, acc_ref):
    t = pl.program_id(0)
    size = jac_ref.shape[0]
    gb = jac_ref.shape[1]
    nb = acc_ref.shape[0]

    @pl.when(t == 0)
    def _init():
        for h in range(xf_ref.shape[0]):
            xf_ref[h, pl.ds(size * gb, (P_PAD - size) * gb), :] = jnp.zeros(((P_PAD - size) * gb, 128), jnp.float32)
        acc_ref[...] = jnp.zeros(acc_ref.shape, jnp.float32)

    halves = xf_ref.shape[0]
    for p in range(size):
        for h in range(halves):
            xf_ref[h, pl.ds(p * gb, gb), :] = jac_ref[p, :, h * 128:(h + 1) * 128].astype(jnp.float32)

    for c in range(gb // GROUP):
        parts = [
            jnp.concatenate([xf_ref[h, pl.ds(c * GROUP + i, P_PAD, stride=gb), :] for h in range(halves)], axis=1)
            for i in range(GROUP)
        ]
        a = jnp.concatenate(parts, axis=0).astype(jnp.bfloat16)
        prod = lax.dot_general(a, a, (((1,), (1,)), ((), ())), preferred_element_type=jnp.float32)
        for i in range(GROUP):
            g = c * GROUP + i
            lane0 = 128 * ((i * P_PAD) // 128)
            sc_ref[pl.ds(g * P_PAD, P_PAD), :] = prod[i * P_PAD:(i + 1) * P_PAD, lane0:lane0 + 128]

    odd = (lax.broadcasted_iota(jnp.int32, (P_PAD, gb), 1) % 2) == 1
    weights = [w_ref[t, b] for b in range(nb)]
    for p in range(size):
        s = sc_ref[pl.ds(p, gb, stride=P_PAD), :]
        tr = s.T
        row = jnp.where(odd, tr[P_PAD:2 * P_PAD], tr[0:P_PAD])
        for b in range(nb):
            acc_ref[b, p] += weights[b] * row

    @pl.when(t == pl.num_programs(0) - 1)
    def _pack():
        offs = row_offsets(size)
        for b in range(nb):
            for p in range(size):
                out_ref[b, pl.ds(offs[p], size - p), :] = acc_ref[b, p, pl.ds(p, size - p), :]


def gram_packed(tiles, weights):
    nt, size, gb, nx = tiles.shape
    nb = weights.shape[1]
    packed_rows = size * (size + 1) // 2
    return pl.pallas_call(
        gram_kernel,
        grid=(nt,),
        in_specs=[
            pl.BlockSpec(memory_space=pltpu.SMEM),
            pl.BlockSpec((None, size, gb, nx), lambda t: (t, 0, 0, 0)),
        ],
        out_specs=pl.BlockSpec((nb, packed_rows, gb), lambda t: (0, 0, 0)),
        out_shape=jax.ShapeDtypeStruct((nb, packed_rows, gb), jnp.float32),
        scratch_shapes=[
            pltpu.VMEM((nx // 128, P_PAD * gb, 128), jnp.float32),
            pltpu.VMEM((gb * P_PAD, 128), jnp.float32),
            pltpu.VMEM((nb, size, P_PAD, gb), jnp.float32),
        ],
        compiler_params=pltpu.CompilerParams(vmem_limit_bytes=48 * 1024 * 1024),
    )(weights, tiles)


def unpack_kernel(packed_ref, out_ref, u_ref):
    nb, size = out_ref.shape[0], out_ref.shape[1]
    offs = row_offsets(size)
    q_id = lax.broadcasted_iota(jnp.int32, (P_PAD, out_ref.shape[3]), 0)
    for b in range(nb):
        for p in range(size):
            u_ref[pl.ds(p * P_PAD + p, size - p), :] = packed_ref[b, pl.ds(offs[p], size - p), :]
        for p in range(size):
            up = u_ref[pl.ds(p * P_PAD, P_PAD), :]
            low = u_ref[pl.ds(p, P_PAD, stride=P_PAD), :]
            full = jnp.where(q_id >= p, up, low)
            out_ref[b, p] = full[0:size]


def unpack(packed, size):
    nb, _, gb = packed.shape
    return pl.pallas_call(
        unpack_kernel,
        in_specs=[pl.BlockSpec(memory_space=pltpu.VMEM)],
        out_specs=pl.BlockSpec(memory_space=pltpu.VMEM),
        out_shape=jax.ShapeDtypeStruct((nb, size, size, gb), jnp.float32),
        scratch_shapes=[pltpu.VMEM((P_PAD * P_PAD, gb), jnp.float32)],
    )(packed)


def local(jac, tile_count, tile_block, tile_pix, residual, direction):
    slot_total = jac.shape[1]
    blocks = direction.shape[0]
    size = jac.shape[2]
    live_count = tile_count[0, 0]
    block_ids = tile_block[0]
    pix_ids = tile_pix[0]
    alive_mask = jnp.arange(slot_total) < live_count
    alive_float = alive_mask.astype(jnp.float32)
    tiles_now = jac[0]
    block_match = block_ids[:, None] == jnp.arange(blocks)[None, :]
    block_hot = (block_match & alive_mask[:, None]).astype(jnp.float32)

    packed_gram = gram_packed(tiles_now, block_hot)
    resid_rows = jnp.take(residual[0], pix_ids, axis=0)
    grad_terms = jnp.einsum(
        "tpgx,tx->tpg", tiles_now, resid_rows, preferred_element_type=jnp.float32
    )
    grad_acc = jnp.sum(block_hot.T[:, :, None, None] * grad_terms[None], axis=1)
    payload = jnp.concatenate([packed_gram, grad_acc], axis=1)
    payload, tiles_now = lax.optimization_barrier((payload, tiles_now))
    summed = lax.psum(payload, "view")
    packed_rows = size * (size + 1) // 2
    gram_sum = unpack(summed, size)
    grad_sum = summed[:, packed_rows:]

    dir_rows = jnp.take(direction, block_ids, axis=0)
    shade_rows = (
        jnp.einsum("tpgx,tpg->tx", tiles_now, dir_rows, preferred_element_type=jnp.float32)
        * alive_float[:, None]
    )
    tagged = jnp.where(alive_mask, pix_ids + 1, 0).astype(jnp.float32)
    all_rows, all_tags = side_by_side((shade_rows, tagged), "gauss", 0, 1)
    own_tags = jnp.where(alive_mask, pix_ids + 1, -1).astype(jnp.float32)
    match_hot = (own_tags[:, None] == all_tags[None, :]).astype(jnp.float32)
    jp_rows = jnp.dot(match_hot, all_rows, precision=lax.Precision.HIGHEST)
    jp_round = jp_rows.astype(jnp.bfloat16)
    curv_terms = jnp.einsum("tpgx,tx->tpg", tiles_now, jp_round, preferred_element_type=jnp.float32)
    curv_acc = jnp.sum(block_hot.T[:, :, None, None] * curv_terms[None], axis=1)
    curv_sum = over_copies(curv_acc, "view")
    return (grad_sum, curv_sum, gram_sum)


def solution(mesh):
    placed = (
        P("view", "gauss", None, None, None),
        P("view", "gauss"),
        P("view", "gauss"),
        P("view", "gauss"),
        P("view", None, None),
        P("gauss", None, None),
    )
    return jax.shard_map(
        local,
        mesh=mesh,
        in_specs=placed,
        out_specs=(P("gauss", None, None), P("gauss", None, None), P("gauss", None, None, None)),
        check_vma=False,
    )
```

```python
import math

import jax
import jax.numpy as jnp
import numpy as np
from jax import lax
from jax.sharding import PartitionSpec as P
from jax.experimental import pallas as pl
from jax.experimental.pallas import tpu as pltpu


def side_by_side(arrays, axis, dim, along):
    widths = [math.prod(a.shape[along:]) for a in arrays]
    both = jnp.concatenate(
        [a.reshape(*a.shape[:along], w) for a, w in zip(arrays, widths)], axis=along
    )
    result = lax.all_gather(both, axis, axis=dim, tiled=True)
    blocks = jnp.split(result, [sum(widths[:k]) for k in range(1, len(widths))], axis=along)
    return tuple(
        (b.reshape(*result.shape[:along], *a.shape[along:]) for a, b in zip(arrays, blocks))
    )


def copy_for_each(array, axis):
    length = lax.axis_size(axis)
    return lax.all_to_all(
        jnp.broadcast_to(array[None], (length, *array.shape)), axis, 0, 0, tiled=True
    )


def over_copies(array, axis):
    everything = copy_for_each(array, axis)
    return jnp.sum(everything, axis=0)


P_PAD = 64
GROUP = 4


def row_offsets(size):
    return [p * size - p * (p - 1) // 2 for p in range(size)]


def gram_kernel(w_ref, jac_ref, out_ref, xf_ref, sc_ref, acc_ref):
    t = pl.program_id(0)
    size = jac_ref.shape[0]
    gb = jac_ref.shape[1]
    nb = acc_ref.shape[0]

    @pl.when(t == 0)
    def _init():
        for h in range(xf_ref.shape[0]):
            xf_ref[h, pl.ds(size * gb, (P_PAD - size) * gb), :] = jnp.zeros(((P_PAD - size) * gb, 128), jnp.float32)
        acc_ref[...] = jnp.zeros(acc_ref.shape, jnp.float32)

    halves = xf_ref.shape[0]
    for p in range(size):
        for h in range(halves):
            xf_ref[h, pl.ds(p * gb, gb), :] = jac_ref[p, :, h * 128:(h + 1) * 128].astype(jnp.float32)

    for c in range(gb // GROUP):
        parts = [
            jnp.concatenate([xf_ref[h, pl.ds(c * GROUP + i, P_PAD, stride=gb), :] for h in range(halves)], axis=1)
            for i in range(GROUP)
        ]
        a = jnp.concatenate(parts, axis=0).astype(jnp.bfloat16)
        prod = lax.dot_general(a, a, (((1,), (1,)), ((), ())), preferred_element_type=jnp.float32)
        for i in range(GROUP):
            g = c * GROUP + i
            lane0 = 128 * ((i * P_PAD) // 128)
            sc_ref[pl.ds(g * P_PAD, P_PAD), :] = prod[i * P_PAD:(i + 1) * P_PAD, lane0:lane0 + 128]

    odd = (lax.broadcasted_iota(jnp.int32, (P_PAD, gb), 1) % 2) == 1
    weights = [w_ref[t, b] for b in range(nb)]
    for p in range(size):
        s = sc_ref[pl.ds(p, gb, stride=P_PAD), :]
        tr = s.T
        row = jnp.where(odd, tr[P_PAD:2 * P_PAD], tr[0:P_PAD])
        for b in range(nb):
            acc_ref[b, p] += weights[b] * row

    @pl.when(t == pl.num_programs(0) - 1)
    def _pack():
        offs = row_offsets(size)
        for b in range(nb):
            for p in range(size):
                out_ref[b, pl.ds(offs[p], size - p), :] = acc_ref[b, p, pl.ds(p, size - p), :]


def gram_packed(tiles, weights):
    nt, size, gb, nx = tiles.shape
    nb = weights.shape[1]
    packed_rows = size * (size + 1) // 2
    return pl.pallas_call(
        gram_kernel,
        grid=(nt,),
        in_specs=[
            pl.BlockSpec(memory_space=pltpu.SMEM),
            pl.BlockSpec((None, size, gb, nx), lambda t: (t, 0, 0, 0)),
        ],
        out_specs=pl.BlockSpec((nb, packed_rows, gb), lambda t: (0, 0, 0)),
        out_shape=jax.ShapeDtypeStruct((nb, packed_rows, gb), jnp.float32),
        scratch_shapes=[
            pltpu.VMEM((nx // 128, P_PAD * gb, 128), jnp.float32),
            pltpu.VMEM((gb * P_PAD, 128), jnp.float32),
            pltpu.VMEM((nb, size, P_PAD, gb), jnp.float32),
        ],
        compiler_params=pltpu.CompilerParams(vmem_limit_bytes=48 * 1024 * 1024),
    )(weights, tiles)


def unpack_kernel(packed_ref, out_ref, u_ref):
    size, nb = out_ref.shape[0], out_ref.shape[2]
    offs = row_offsets(size)
    q_id = lax.broadcasted_iota(jnp.int32, (P_PAD, out_ref.shape[3]), 0)
    for b in range(nb):
        for p in range(size):
            u_ref[b, pl.ds(p * P_PAD + p, size - p), :] = packed_ref[b, pl.ds(offs[p], size - p), :]
    for p in range(size):
        rows = []
        for b in range(nb):
            up = u_ref[b, pl.ds(p * P_PAD, P_PAD), :]
            low = u_ref[b, pl.ds(p, P_PAD, stride=P_PAD), :]
            rows.append(jnp.where(q_id >= p, up, low)[0:size])
        out_ref[p] = jnp.stack(rows, axis=1)


def unpack(packed, size):
    nb, _, gb = packed.shape
    full = pl.pallas_call(
        unpack_kernel,
        in_specs=[pl.BlockSpec(memory_space=pltpu.VMEM)],
        out_specs=pl.BlockSpec(memory_space=pltpu.VMEM),
        out_shape=jax.ShapeDtypeStruct((size, size, nb, gb), jnp.float32),
        scratch_shapes=[pltpu.VMEM((nb, P_PAD * P_PAD, gb), jnp.float32)],
    )(packed)
    return jnp.transpose(full, (2, 0, 1, 3))


def local(jac, tile_count, tile_block, tile_pix, residual, direction):
    slot_total = jac.shape[1]
    blocks = direction.shape[0]
    size = jac.shape[2]
    live_count = tile_count[0, 0]
    block_ids = tile_block[0]
    pix_ids = tile_pix[0]
    alive_mask = jnp.arange(slot_total) < live_count
    alive_float = alive_mask.astype(jnp.float32)
    tiles_now = jac[0]
    block_match = block_ids[:, None] == jnp.arange(blocks)[None, :]
    block_hot = (block_match & alive_mask[:, None]).astype(jnp.float32)

    packed_gram = gram_packed(tiles_now, block_hot)
    resid_rows = jnp.take(residual[0], pix_ids, axis=0)
    grad_terms = jnp.einsum(
        "tpgx,tx->tpg", tiles_now, resid_rows, preferred_element_type=jnp.float32
    )
    grad_acc = jnp.sum(block_hot.T[:, :, None, None] * grad_terms[None], axis=1)
    payload = jnp.concatenate([packed_gram, grad_acc], axis=1)
    payload, tiles_now = lax.optimization_barrier((payload, tiles_now))
    summed = lax.psum(payload, "view")
    packed_rows = size * (size + 1) // 2
    gram_sum = unpack(summed, size)
    grad_sum = summed[:, packed_rows:]

    dir_rows = jnp.take(direction, block_ids, axis=0)
    shade_rows = (
        jnp.einsum("tpgx,tpg->tx", tiles_now, dir_rows, preferred_element_type=jnp.float32)
        * alive_float[:, None]
    )
    tagged = jnp.where(alive_mask, pix_ids + 1, 0).astype(jnp.float32)
    all_rows, all_tags = side_by_side((shade_rows, tagged), "gauss", 0, 1)
    own_tags = jnp.where(alive_mask, pix_ids + 1, -1).astype(jnp.float32)
    match_hot = (own_tags[:, None] == all_tags[None, :]).astype(jnp.float32)
    jp_rows = jnp.dot(match_hot, all_rows, precision=lax.Precision.HIGHEST)
    jp_round = jp_rows.astype(jnp.bfloat16)
    curv_terms = jnp.einsum("tpgx,tx->tpg", tiles_now, jp_round, preferred_element_type=jnp.float32)
    curv_acc = jnp.sum(block_hot.T[:, :, None, None] * curv_terms[None], axis=1)
    curv_sum = over_copies(curv_acc, "view")
    return (grad_sum, curv_sum, gram_sum)


def solution(mesh):
    placed = (
        P("view", "gauss", None, None, None),
        P("view", "gauss"),
        P("view", "gauss"),
        P("view", "gauss"),
        P("view", None, None),
        P("gauss", None, None),
    )
    return jax.shard_map(
        local,
        mesh=mesh,
        in_specs=placed,
        out_specs=(P("gauss", None, None), P("gauss", None, None), P("gauss", None, None, None)),
        check_vma=False,
    )
```

```python
import math

import jax
import jax.numpy as jnp
import numpy as np
from jax import lax
from jax.sharding import PartitionSpec as P
from jax.experimental import pallas as pl
from jax.experimental.pallas import tpu as pltpu


def side_by_side(arrays, axis, dim, along):
    widths = [math.prod(a.shape[along:]) for a in arrays]
    both = jnp.concatenate(
        [a.reshape(*a.shape[:along], w) for a, w in zip(arrays, widths)], axis=along
    )
    result = lax.all_gather(both, axis, axis=dim, tiled=True)
    blocks = jnp.split(result, [sum(widths[:k]) for k in range(1, len(widths))], axis=along)
    return tuple(
        (b.reshape(*result.shape[:along], *a.shape[along:]) for a, b in zip(arrays, blocks))
    )


def copy_for_each(array, axis):
    length = lax.axis_size(axis)
    return lax.all_to_all(
        jnp.broadcast_to(array[None], (length, *array.shape)), axis, 0, 0, tiled=True
    )


def over_copies(array, axis):
    everything = copy_for_each(array, axis)
    return jnp.sum(everything, axis=0)


P_PAD = 64
GROUP = 4


def row_offsets(size):
    return [p * size - p * (p - 1) // 2 for p in range(size)]


def gram_kernel(w_ref, jac_ref, out_ref, xf_ref, sc_ref, acc_ref):
    t = pl.program_id(0)
    size = jac_ref.shape[0]
    gb = jac_ref.shape[1]
    nb = acc_ref.shape[0]

    @pl.when(t == 0)
    def _init():
        for h in range(xf_ref.shape[0]):
            xf_ref[h, pl.ds(size * gb, (P_PAD - size) * gb), :] = jnp.zeros(((P_PAD - size) * gb, 128), jnp.float32)
        acc_ref[...] = jnp.zeros(acc_ref.shape, jnp.float32)

    halves = xf_ref.shape[0]
    for p in range(size):
        for h in range(halves):
            xf_ref[h, pl.ds(p * gb, gb), :] = jac_ref[p, :, h * 128:(h + 1) * 128].astype(jnp.float32)

    for c in range(gb // GROUP):
        parts = [
            jnp.concatenate([xf_ref[h, pl.ds(c * GROUP + i, P_PAD, stride=gb), :] for h in range(halves)], axis=1)
            for i in range(GROUP)
        ]
        a = jnp.concatenate(parts, axis=0).astype(jnp.bfloat16)
        prod = lax.dot_general(a, a, (((1,), (1,)), ((), ())), preferred_element_type=jnp.float32)
        for i in range(GROUP):
            g = c * GROUP + i
            lane0 = 128 * ((i * P_PAD) // 128)
            sc_ref[pl.ds(g * P_PAD, P_PAD), :] = prod[i * P_PAD:(i + 1) * P_PAD, lane0:lane0 + 128]

    odd = (lax.broadcasted_iota(jnp.int32, (P_PAD, gb), 1) % 2) == 1
    weights = [w_ref[t, b] for b in range(nb)]
    for p in range(size):
        s = sc_ref[pl.ds(p, gb, stride=P_PAD), :]
        tr = s.T
        row = jnp.where(odd, tr[P_PAD:2 * P_PAD], tr[0:P_PAD])
        for b in range(nb):
            acc_ref[b, p] += weights[b] * row

    @pl.when(t == pl.num_programs(0) - 1)
    def _pack():
        offs = row_offsets(size)
        for b in range(nb):
            for p in range(size):
                out_ref[b, pl.ds(offs[p], size - p), :] = acc_ref[b, p, pl.ds(p, size - p), :]


def gram_packed(tiles, weights):
    nt, size, gb, nx = tiles.shape
    nb = weights.shape[1]
    packed_rows = size * (size + 1) // 2
    return pl.pallas_call(
        gram_kernel,
        grid=(nt,),
        in_specs=[
            pl.BlockSpec(memory_space=pltpu.SMEM),
            pl.BlockSpec((None, size, gb, nx), lambda t: (t, 0, 0, 0)),
        ],
        out_specs=pl.BlockSpec((nb, packed_rows, gb), lambda t: (0, 0, 0)),
        out_shape=jax.ShapeDtypeStruct((nb, packed_rows, gb), jnp.float32),
        scratch_shapes=[
            pltpu.VMEM((nx // 128, P_PAD * gb, 128), jnp.float32),
            pltpu.VMEM((gb * P_PAD, 128), jnp.float32),
            pltpu.VMEM((nb, size, P_PAD, gb), jnp.float32),
        ],
        compiler_params=pltpu.CompilerParams(vmem_limit_bytes=48 * 1024 * 1024),
    )(weights, tiles)


def unpack_kernel(packed_ref, out_ref, u_ref):
    size, nb = out_ref.shape[0], out_ref.shape[2]
    offs = row_offsets(size)
    q_id = lax.broadcasted_iota(jnp.int32, (P_PAD, out_ref.shape[3]), 0)
    for b in range(nb):
        for p in range(size):
            u_ref[b, pl.ds(p * P_PAD + p, size - p), :] = packed_ref[b, pl.ds(offs[p], size - p), :]
    for p in range(size):
        rows = []
        for b in range(nb):
            up = u_ref[b, pl.ds(p * P_PAD, P_PAD), :]
            low = u_ref[b, pl.ds(p, P_PAD, stride=P_PAD), :]
            rows.append(jnp.where(q_id >= p, up, low)[0:size])
        out_ref[p] = jnp.stack(rows, axis=1)


def unpack(packed, size):
    nb, _, gb = packed.shape
    full = pl.pallas_call(
        unpack_kernel,
        in_specs=[pl.BlockSpec(memory_space=pltpu.VMEM)],
        out_specs=pl.BlockSpec(memory_space=pltpu.VMEM),
        out_shape=jax.ShapeDtypeStruct((size, size, nb, gb), jnp.float32),
        scratch_shapes=[pltpu.VMEM((nb, P_PAD * P_PAD, gb), jnp.float32)],
    )(packed)
    return jnp.transpose(full, (2, 0, 1, 3))


def local(jac, tile_count, tile_block, tile_pix, residual, direction):
    slot_total = jac.shape[1]
    blocks = direction.shape[0]
    size = jac.shape[2]
    live_count = tile_count[0, 0]
    block_ids = tile_block[0]
    pix_ids = tile_pix[0]
    alive_mask = jnp.arange(slot_total) < live_count
    alive_float = alive_mask.astype(jnp.float32)
    tiles_now = jac[0]
    block_match = block_ids[:, None] == jnp.arange(blocks)[None, :]
    block_hot = (block_match & alive_mask[:, None]).astype(jnp.float32)

    packed_gram = gram_packed(tiles_now, block_hot)
    packed_gram, tiles_now = lax.optimization_barrier((packed_gram, tiles_now))
    summed = lax.psum(packed_gram, "view")
    gram_sum = unpack(summed, size)

    dir_rows = jnp.take(direction, block_ids, axis=0)
    shade_rows = (
        jnp.einsum("tpgx,tpg->tx", tiles_now, dir_rows, preferred_element_type=jnp.float32)
        * alive_float[:, None]
    )
    tagged = jnp.where(alive_mask, pix_ids + 1, 0).astype(jnp.float32)
    all_rows, all_tags = side_by_side((shade_rows, tagged), "gauss", 0, 1)
    own_tags = jnp.where(alive_mask, pix_ids + 1, -1).astype(jnp.float32)
    match_hot = (own_tags[:, None] == all_tags[None, :]).astype(jnp.float32)
    jp_rows = jnp.dot(match_hot, all_rows, precision=lax.Precision.HIGHEST)
    jp_round = jp_rows.astype(jnp.bfloat16)
    curv_terms = jnp.einsum("tpgx,tx->tpg", tiles_now, jp_round, preferred_element_type=jnp.float32)
    curv_acc = jnp.sum(block_hot.T[:, :, None, None] * curv_terms[None], axis=1)
    resid_rows = jnp.take(residual[0], pix_ids, axis=0)
    grad_terms = jnp.einsum(
        "tpgx,tx->tpg", tiles_now, resid_rows, preferred_element_type=jnp.float32
    )
    grad_acc = jnp.sum(block_hot.T[:, :, None, None] * grad_terms[None], axis=1)
    both_sum = over_copies(jnp.stack([grad_acc, curv_acc]), "view")
    return (both_sum[0], both_sum[1], gram_sum)


def solution(mesh):
    placed = (
        P("view", "gauss", None, None, None),
        P("view", "gauss"),
        P("view", "gauss"),
        P("view", "gauss"),
        P("view", None, None),
        P("gauss", None, None),
    )
    return jax.shard_map(
        local,
        mesh=mesh,
        in_specs=placed,
        out_specs=(P("gauss", None, None), P("gauss", None, None), P("gauss", None, None, None)),
        check_vma=False,
    )
```

```python
import math

import jax
import jax.numpy as jnp
import numpy as np
from jax import lax
from jax.sharding import PartitionSpec as P
from jax.experimental import pallas as pl
from jax.experimental.pallas import tpu as pltpu


def side_by_side(arrays, axis, dim, along):
    widths = [math.prod(a.shape[along:]) for a in arrays]
    both = jnp.concatenate(
        [a.reshape(*a.shape[:along], w) for a, w in zip(arrays, widths)], axis=along
    )
    result = copy_for_each(both, axis).reshape(-1, *both.shape[1:])
    blocks = jnp.split(result, [sum(widths[:k]) for k in range(1, len(widths))], axis=along)
    return tuple(
        (b.reshape(*result.shape[:along], *a.shape[along:]) for a, b in zip(arrays, blocks))
    )


def copy_for_each(array, axis):
    length = lax.axis_size(axis)
    return lax.all_to_all(
        jnp.broadcast_to(array[None], (length, *array.shape)), axis, 0, 0, tiled=True
    )


def over_copies(array, axis):
    everything = copy_for_each(array, axis)
    return jnp.sum(everything, axis=0)


P_PAD = 64
GROUP = 4


def row_offsets(size):
    return [p * size - p * (p - 1) // 2 for p in range(size)]


def gram_kernel(w_ref, jac_ref, out_ref, xf_ref, sc_ref, acc_ref):
    t = pl.program_id(0)
    size = jac_ref.shape[0]
    gb = jac_ref.shape[1]
    nb = acc_ref.shape[0]

    @pl.when(t == 0)
    def _init():
        for h in range(xf_ref.shape[0]):
            xf_ref[h, pl.ds(size * gb, (P_PAD - size) * gb), :] = jnp.zeros(((P_PAD - size) * gb, 128), jnp.float32)
        acc_ref[...] = jnp.zeros(acc_ref.shape, jnp.float32)

    halves = xf_ref.shape[0]
    for p in range(size):
        for h in range(halves):
            xf_ref[h, pl.ds(p * gb, gb), :] = jac_ref[p, :, h * 128:(h + 1) * 128].astype(jnp.float32)

    for c in range(gb // GROUP):
        parts = [
            jnp.concatenate([xf_ref[h, pl.ds(c * GROUP + i, P_PAD, stride=gb), :] for h in range(halves)], axis=1)
            for i in range(GROUP)
        ]
        a = jnp.concatenate(parts, axis=0).astype(jnp.bfloat16)
        prod = lax.dot_general(a, a, (((1,), (1,)), ((), ())), preferred_element_type=jnp.float32)
        for i in range(GROUP):
            g = c * GROUP + i
            lane0 = 128 * ((i * P_PAD) // 128)
            sc_ref[pl.ds(g * P_PAD, P_PAD), :] = prod[i * P_PAD:(i + 1) * P_PAD, lane0:lane0 + 128]

    odd = (lax.broadcasted_iota(jnp.int32, (P_PAD, gb), 1) % 2) == 1
    weights = [w_ref[t, b] for b in range(nb)]
    for p in range(size):
        s = sc_ref[pl.ds(p, gb, stride=P_PAD), :]
        tr = s.T
        row = jnp.where(odd, tr[P_PAD:2 * P_PAD], tr[0:P_PAD])
        for b in range(nb):
            acc_ref[b, p] += weights[b] * row

    @pl.when(t == pl.num_programs(0) - 1)
    def _pack():
        offs = row_offsets(size)
        for b in range(nb):
            for p in range(size):
                out_ref[b, pl.ds(offs[p], size - p), :] = acc_ref[b, p, pl.ds(p, size - p), :]


def gram_packed(tiles, weights):
    nt, size, gb, nx = tiles.shape
    nb = weights.shape[1]
    packed_rows = size * (size + 1) // 2
    return pl.pallas_call(
        gram_kernel,
        grid=(nt,),
        in_specs=[
            pl.BlockSpec(memory_space=pltpu.SMEM),
            pl.BlockSpec((None, size, gb, nx), lambda t: (t, 0, 0, 0)),
        ],
        out_specs=pl.BlockSpec((nb, packed_rows, gb), lambda t: (0, 0, 0)),
        out_shape=jax.ShapeDtypeStruct((nb, packed_rows, gb), jnp.float32),
        scratch_shapes=[
            pltpu.VMEM((nx // 128, P_PAD * gb, 128), jnp.float32),
            pltpu.VMEM((gb * P_PAD, 128), jnp.float32),
            pltpu.VMEM((nb, size, P_PAD, gb), jnp.float32),
        ],
        compiler_params=pltpu.CompilerParams(vmem_limit_bytes=48 * 1024 * 1024),
    )(weights, tiles)


def unpack_kernel(packed_ref, out_ref, u_ref):
    size, nb = out_ref.shape[0], out_ref.shape[2]
    offs = row_offsets(size)
    q_id = lax.broadcasted_iota(jnp.int32, (P_PAD, out_ref.shape[3]), 0)
    for b in range(nb):
        for p in range(size):
            u_ref[b, pl.ds(p * P_PAD + p, size - p), :] = packed_ref[b, pl.ds(offs[p], size - p), :]
    for p in range(size):
        rows = []
        for b in range(nb):
            up = u_ref[b, pl.ds(p * P_PAD, P_PAD), :]
            low = u_ref[b, pl.ds(p, P_PAD, stride=P_PAD), :]
            rows.append(jnp.where(q_id >= p, up, low)[0:size])
        out_ref[p] = jnp.stack(rows, axis=1)


def unpack(packed, size):
    nb, _, gb = packed.shape
    full = pl.pallas_call(
        unpack_kernel,
        in_specs=[pl.BlockSpec(memory_space=pltpu.VMEM)],
        out_specs=pl.BlockSpec(memory_space=pltpu.VMEM),
        out_shape=jax.ShapeDtypeStruct((size, size, nb, gb), jnp.float32),
        scratch_shapes=[pltpu.VMEM((nb, P_PAD * P_PAD, gb), jnp.float32)],
    )(packed)
    return jnp.transpose(full, (2, 0, 1, 3))


def local(jac, tile_count, tile_block, tile_pix, residual, direction):
    slot_total = jac.shape[1]
    blocks = direction.shape[0]
    size = jac.shape[2]
    live_count = tile_count[0, 0]
    block_ids = tile_block[0]
    pix_ids = tile_pix[0]
    alive_mask = jnp.arange(slot_total) < live_count
    alive_float = alive_mask.astype(jnp.float32)
    tiles_now = jac[0]
    block_match = block_ids[:, None] == jnp.arange(blocks)[None, :]
    block_hot = (block_match & alive_mask[:, None]).astype(jnp.float32)

    packed_gram = gram_packed(tiles_now, block_hot)
    packed_gram, tiles_now = lax.optimization_barrier((packed_gram, tiles_now))
    summed = lax.psum(packed_gram, "view")
    gram_sum = unpack(summed, size)

    dir_rows = jnp.take(direction, block_ids, axis=0)
    shade_rows = (
        jnp.einsum("tpgx,tpg->tx", tiles_now, dir_rows, preferred_element_type=jnp.float32)
        * alive_float[:, None]
    )
    tagged = jnp.where(alive_mask, pix_ids + 1, 0).astype(jnp.float32)
    all_rows, all_tags = side_by_side((shade_rows, tagged), "gauss", 0, 1)
    own_tags = jnp.where(alive_mask, pix_ids + 1, -1).astype(jnp.float32)
    match_hot = (own_tags[:, None] == all_tags[None, :]).astype(jnp.float32)
    jp_rows = jnp.dot(match_hot, all_rows, precision=lax.Precision.HIGHEST)
    jp_round = jp_rows.astype(jnp.bfloat16)
    curv_terms = jnp.einsum("tpgx,tx->tpg", tiles_now, jp_round, preferred_element_type=jnp.float32)
    curv_acc = jnp.sum(block_hot.T[:, :, None, None] * curv_terms[None], axis=1)
    resid_rows = jnp.take(residual[0], pix_ids, axis=0)
    grad_terms = jnp.einsum(
        "tpgx,tx->tpg", tiles_now, resid_rows, preferred_element_type=jnp.float32
    )
    grad_acc = jnp.sum(block_hot.T[:, :, None, None] * grad_terms[None], axis=1)
    both_sum = over_copies(jnp.stack([grad_acc, curv_acc]), "view")
    return (both_sum[0], both_sum[1], gram_sum)


def solution(mesh):
    placed = (
        P("view", "gauss", None, None, None),
        P("view", "gauss"),
        P("view", "gauss"),
        P("view", "gauss"),
        P("view", None, None),
        P("gauss", None, None),
    )
    return jax.shard_map(
        local,
        mesh=mesh,
        in_specs=placed,
        out_specs=(P("gauss", None, None), P("gauss", None, None), P("gauss", None, None, None)),
        check_vma=False,
    )
```

```python
import math

import jax
import jax.numpy as jnp
import numpy as np
from jax import lax
from jax.sharding import PartitionSpec as P
from jax.experimental import pallas as pl
from jax.experimental.pallas import tpu as pltpu


def side_by_side(arrays, axis, dim, along):
    widths = [math.prod(a.shape[along:]) for a in arrays]
    both = jnp.concatenate(
        [a.reshape(*a.shape[:along], w) for a, w in zip(arrays, widths)], axis=along
    )
    result = copy_for_each(both, axis).reshape(-1, *both.shape[1:])
    blocks = jnp.split(result, [sum(widths[:k]) for k in range(1, len(widths))], axis=along)
    return tuple(
        (b.reshape(*result.shape[:along], *a.shape[along:]) for a, b in zip(arrays, blocks))
    )


def copy_for_each(array, axis):
    length = lax.axis_size(axis)
    return lax.all_to_all(
        jnp.broadcast_to(array[None], (length, *array.shape)), axis, 0, 0, tiled=True
    )


def over_copies(array, axis):
    everything = copy_for_each(array, axis)
    return jnp.sum(everything, axis=0)


P_PAD = 64
GROUP = 2


def row_offsets(size):
    return [p * size - p * (p - 1) // 2 for p in range(size)]


def gram_kernel(w_ref, jac_ref, out_ref, xf_ref, sc_ref, acc_ref):
    t = pl.program_id(0)
    size = jac_ref.shape[0]
    gb = jac_ref.shape[1]
    nb = acc_ref.shape[0]

    @pl.when(t == 0)
    def _init():
        for h in range(xf_ref.shape[0]):
            xf_ref[h, pl.ds(size * gb, (P_PAD - size) * gb), :] = jnp.zeros(((P_PAD - size) * gb, 128), jnp.float32)
        acc_ref[...] = jnp.zeros(acc_ref.shape, jnp.float32)

    halves = xf_ref.shape[0]
    for p in range(size):
        for h in range(halves):
            xf_ref[h, pl.ds(p * gb, gb), :] = jac_ref[p, :, h * 128:(h + 1) * 128].astype(jnp.float32)

    for c in range(gb // GROUP):
        parts = [
            jnp.concatenate([xf_ref[h, pl.ds(c * GROUP + i, P_PAD, stride=gb), :] for h in range(halves)], axis=1)
            for i in range(GROUP)
        ]
        a = jnp.concatenate(parts, axis=0).astype(jnp.bfloat16)
        prod = lax.dot_general(a, a, (((1,), (1,)), ((), ())), preferred_element_type=jnp.float32)
        for i in range(GROUP):
            g = c * GROUP + i
            lane0 = 128 * ((i * P_PAD) // 128)
            sc_ref[pl.ds(g * P_PAD, P_PAD), :] = prod[i * P_PAD:(i + 1) * P_PAD, lane0:lane0 + 128]

    odd = (lax.broadcasted_iota(jnp.int32, (P_PAD, gb), 1) % 2) == 1
    weights = [w_ref[t, b] for b in range(nb)]
    for p in range(size):
        s = sc_ref[pl.ds(p, gb, stride=P_PAD), :]
        tr = s.T
        row = jnp.where(odd, tr[P_PAD:2 * P_PAD], tr[0:P_PAD])
        for b in range(nb):
            acc_ref[b, p] += weights[b] * row

    @pl.when(t == pl.num_programs(0) - 1)
    def _pack():
        offs = row_offsets(size)
        for b in range(nb):
            for p in range(size):
                out_ref[b, pl.ds(offs[p], size - p), :] = acc_ref[b, p, pl.ds(p, size - p), :]


def gram_packed(tiles, weights):
    nt, size, gb, nx = tiles.shape
    nb = weights.shape[1]
    packed_rows = size * (size + 1) // 2
    return pl.pallas_call(
        gram_kernel,
        grid=(nt,),
        in_specs=[
            pl.BlockSpec(memory_space=pltpu.SMEM),
            pl.BlockSpec((None, size, gb, nx), lambda t: (t, 0, 0, 0)),
        ],
        out_specs=pl.BlockSpec((nb, packed_rows, gb), lambda t: (0, 0, 0)),
        out_shape=jax.ShapeDtypeStruct((nb, packed_rows, gb), jnp.float32),
        scratch_shapes=[
            pltpu.VMEM((nx // 128, P_PAD * gb, 128), jnp.float32),
            pltpu.VMEM((gb * P_PAD, 128), jnp.float32),
            pltpu.VMEM((nb, size, P_PAD, gb), jnp.float32),
        ],
        compiler_params=pltpu.CompilerParams(vmem_limit_bytes=48 * 1024 * 1024),
    )(weights, tiles)


def unpack_kernel(packed_ref, out_ref, u_ref):
    size, nb = out_ref.shape[0], out_ref.shape[2]
    offs = row_offsets(size)
    q_id = lax.broadcasted_iota(jnp.int32, (P_PAD, out_ref.shape[3]), 0)
    for b in range(nb):
        for p in range(size):
            u_ref[b, pl.ds(p * P_PAD + p, size - p), :] = packed_ref[b, pl.ds(offs[p], size - p), :]
    for p in range(size):
        rows = []
        for b in range(nb):
            up = u_ref[b, pl.ds(p * P_PAD, P_PAD), :]
            low = u_ref[b, pl.ds(p, P_PAD, stride=P_PAD), :]
            rows.append(jnp.where(q_id >= p, up, low)[0:size])
        out_ref[p] = jnp.stack(rows, axis=1)


def unpack(packed, size):
    nb, _, gb = packed.shape
    full = pl.pallas_call(
        unpack_kernel,
        in_specs=[pl.BlockSpec(memory_space=pltpu.VMEM)],
        out_specs=pl.BlockSpec(memory_space=pltpu.VMEM),
        out_shape=jax.ShapeDtypeStruct((size, size, nb, gb), jnp.float32),
        scratch_shapes=[pltpu.VMEM((nb, P_PAD * P_PAD, gb), jnp.float32)],
    )(packed)
    return jnp.transpose(full, (2, 0, 1, 3))


def local(jac, tile_count, tile_block, tile_pix, residual, direction):
    slot_total = jac.shape[1]
    blocks = direction.shape[0]
    size = jac.shape[2]
    live_count = tile_count[0, 0]
    block_ids = tile_block[0]
    pix_ids = tile_pix[0]
    alive_mask = jnp.arange(slot_total) < live_count
    alive_float = alive_mask.astype(jnp.float32)
    tiles_now = jac[0]
    block_match = block_ids[:, None] == jnp.arange(blocks)[None, :]
    block_hot = (block_match & alive_mask[:, None]).astype(jnp.float32)

    packed_gram = gram_packed(tiles_now, block_hot)
    packed_gram, tiles_now = lax.optimization_barrier((packed_gram, tiles_now))
    summed = lax.psum(packed_gram, "view")
    gram_sum = unpack(summed, size)

    dir_rows = jnp.take(direction, block_ids, axis=0)
    shade_rows = (
        jnp.einsum("tpgx,tpg->tx", tiles_now, dir_rows, preferred_element_type=jnp.float32)
        * alive_float[:, None]
    )
    tagged = jnp.where(alive_mask, pix_ids + 1, 0).astype(jnp.float32)
    all_rows, all_tags = side_by_side((shade_rows, tagged), "gauss", 0, 1)
    own_tags = jnp.where(alive_mask, pix_ids + 1, -1).astype(jnp.float32)
    match_hot = (own_tags[:, None] == all_tags[None, :]).astype(jnp.float32)
    jp_rows = jnp.dot(match_hot, all_rows, precision=lax.Precision.HIGHEST)
    jp_round = jp_rows.astype(jnp.bfloat16)
    curv_terms = jnp.einsum("tpgx,tx->tpg", tiles_now, jp_round, preferred_element_type=jnp.float32)
    curv_acc = jnp.sum(block_hot.T[:, :, None, None] * curv_terms[None], axis=1)
    resid_rows = jnp.take(residual[0], pix_ids, axis=0)
    grad_terms = jnp.einsum(
        "tpgx,tx->tpg", tiles_now, resid_rows, preferred_element_type=jnp.float32
    )
    grad_acc = jnp.sum(block_hot.T[:, :, None, None] * grad_terms[None], axis=1)
    both_sum = over_copies(jnp.stack([grad_acc, curv_acc]), "view")
    return (both_sum[0], both_sum[1], gram_sum)


def solution(mesh):
    placed = (
        P("view", "gauss", None, None, None),
        P("view", "gauss"),
        P("view", "gauss"),
        P("view", "gauss"),
        P("view", None, None),
        P("gauss", None, None),
    )
    return jax.shard_map(
        local,
        mesh=mesh,
        in_specs=placed,
        out_specs=(P("gauss", None, None), P("gauss", None, None), P("gauss", None, None, None)),
        check_vma=False,
    )
```

```python
import math

import jax
import jax.numpy as jnp
import numpy as np
from jax import lax
from jax.sharding import PartitionSpec as P
from jax.experimental import pallas as pl
from jax.experimental.pallas import tpu as pltpu


def side_by_side(arrays, axis, dim, along):
    widths = [math.prod(a.shape[along:]) for a in arrays]
    both = jnp.concatenate(
        [a.reshape(*a.shape[:along], w) for a, w in zip(arrays, widths)], axis=along
    )
    result = copy_for_each(both, axis).reshape(-1, *both.shape[1:])
    blocks = jnp.split(result, [sum(widths[:k]) for k in range(1, len(widths))], axis=along)
    return tuple(
        (b.reshape(*result.shape[:along], *a.shape[along:]) for a, b in zip(arrays, blocks))
    )


def copy_for_each(array, axis):
    length = lax.axis_size(axis)
    return lax.all_to_all(
        jnp.broadcast_to(array[None], (length, *array.shape)), axis, 0, 0, tiled=True
    )


def over_copies(array, axis):
    everything = copy_for_each(array, axis)
    return jnp.sum(everything, axis=0)


P_PAD = 64
GROUP = 4


def row_offsets(size):
    return [p * size - p * (p - 1) // 2 for p in range(size)]


def gram_kernel(w_ref, jac_ref, out_ref, xf_ref, sc_ref, acc_ref):
    t = pl.program_id(0)
    size = jac_ref.shape[0]
    gb = jac_ref.shape[1]
    nb = acc_ref.shape[0]

    @pl.when(t == 0)
    def _init():
        for h in range(xf_ref.shape[0]):
            xf_ref[h, pl.ds(size * gb, (P_PAD - size) * gb), :] = jnp.zeros(((P_PAD - size) * gb, 128), jnp.float32)
        acc_ref[...] = jnp.zeros(acc_ref.shape, jnp.float32)

    halves = xf_ref.shape[0]
    for p in range(size):
        for h in range(halves):
            xf_ref[h, pl.ds(p * gb, gb), :] = jac_ref[p, :, h * 128:(h + 1) * 128].astype(jnp.float32)

    for c in range(gb // GROUP):
        parts = [
            jnp.concatenate([xf_ref[h, pl.ds(c * GROUP + i, P_PAD, stride=gb), :] for h in range(halves)], axis=1)
            for i in range(GROUP)
        ]
        a = jnp.concatenate(parts, axis=0).astype(jnp.bfloat16)
        prod = lax.dot_general(a, a, (((1,), (1,)), ((), ())), preferred_element_type=jnp.float32)
        for i in range(GROUP):
            g = c * GROUP + i
            lane0 = 128 * ((i * P_PAD) // 128)
            sc_ref[pl.ds(g * P_PAD, P_PAD), :] = prod[i * P_PAD:(i + 1) * P_PAD, lane0:lane0 + 128]

    odd = (lax.broadcasted_iota(jnp.int32, (P_PAD, gb), 1) % 2) == 1
    weights = [w_ref[t, b] for b in range(nb)]
    for p in range(size):
        s = sc_ref[pl.ds(p, gb, stride=P_PAD), :]
        tr = s.T
        row = jnp.where(odd, tr[P_PAD:2 * P_PAD], tr[0:P_PAD])
        for b in range(nb):
            acc_ref[b, p] += weights[b] * row

    @pl.when(t == pl.num_programs(0) - 1)
    def _pack():
        offs = row_offsets(size)
        for b in range(nb):
            for p in range(size):
                out_ref[b, pl.ds(offs[p], size - p), :] = acc_ref[b, p, pl.ds(p, size - p), :]


def gram_packed(tiles, weights):
    nt, size, gb, nx = tiles.shape
    nb = weights.shape[1]
    packed_rows = size * (size + 1) // 2
    return pl.pallas_call(
        gram_kernel,
        grid=(nt,),
        in_specs=[
            pl.BlockSpec(memory_space=pltpu.SMEM),
            pl.BlockSpec((None, size, gb, nx), lambda t: (t, 0, 0, 0)),
        ],
        out_specs=pl.BlockSpec((nb, packed_rows, gb), lambda t: (0, 0, 0)),
        out_shape=jax.ShapeDtypeStruct((nb, packed_rows, gb), jnp.float32),
        scratch_shapes=[
            pltpu.VMEM((nx // 128, P_PAD * gb, 128), jnp.float32),
            pltpu.VMEM((gb * P_PAD, 128), jnp.float32),
            pltpu.VMEM((nb, size, P_PAD, gb), jnp.float32),
        ],
        compiler_params=pltpu.CompilerParams(vmem_limit_bytes=48 * 1024 * 1024),
    )(weights, tiles)


ROW_CHUNK = 8


def unpack_kernel(packed_ref, out_ref, u_ref):
    step = pl.program_id(0)
    size, nb = out_ref.shape[1], out_ref.shape[2]
    offs = row_offsets(size)
    q_id = lax.broadcasted_iota(jnp.int32, (P_PAD, out_ref.shape[3]), 0)

    @pl.when(step == 0)
    def _fill():
        for b in range(nb):
            for p in range(size):
                u_ref[b, pl.ds(p * P_PAD + p, size - p), :] = packed_ref[b, pl.ds(offs[p], size - p), :]

    for c in range(pl.cdiv(size, ROW_CHUNK)):
        @pl.when(step == c)
        def _rows():
            for p in range(c * ROW_CHUNK, min(size, (c + 1) * ROW_CHUNK)):
                rows = []
                for b in range(nb):
                    up = u_ref[b, pl.ds(p * P_PAD, P_PAD), :]
                    low = u_ref[b, pl.ds(p, P_PAD, stride=P_PAD), :]
                    rows.append(jnp.where(q_id >= p, up, low)[0:size])
                out_ref[p - c * ROW_CHUNK] = jnp.stack(rows, axis=1)


def unpack(packed, size):
    nb, rows, gb = packed.shape
    full = pl.pallas_call(
        unpack_kernel,
        grid=(pl.cdiv(size, ROW_CHUNK),),
        in_specs=[pl.BlockSpec((nb, rows, gb), lambda i: (0, 0, 0))],
        out_specs=pl.BlockSpec((ROW_CHUNK, size, nb, gb), lambda i: (i, 0, 0, 0)),
        out_shape=jax.ShapeDtypeStruct((size, size, nb, gb), jnp.float32),
        scratch_shapes=[pltpu.VMEM((nb, P_PAD * P_PAD, gb), jnp.float32)],
    )(packed)
    return jnp.transpose(full, (2, 0, 1, 3))


def local(jac, tile_count, tile_block, tile_pix, residual, direction):
    slot_total = jac.shape[1]
    blocks = direction.shape[0]
    size = jac.shape[2]
    live_count = tile_count[0, 0]
    block_ids = tile_block[0]
    pix_ids = tile_pix[0]
    alive_mask = jnp.arange(slot_total) < live_count
    alive_float = alive_mask.astype(jnp.float32)
    tiles_now = jac[0]
    block_match = block_ids[:, None] == jnp.arange(blocks)[None, :]
    block_hot = (block_match & alive_mask[:, None]).astype(jnp.float32)

    packed_gram = gram_packed(tiles_now, block_hot)
    packed_gram, tiles_now = lax.optimization_barrier((packed_gram, tiles_now))
    summed = lax.psum(packed_gram, "view")
    gram_sum = unpack(summed, size)

    dir_rows = jnp.take(direction, block_ids, axis=0)
    shade_rows = (
        jnp.einsum("tpgx,tpg->tx", tiles_now, dir_rows, preferred_element_type=jnp.float32)
        * alive_float[:, None]
    )
    tagged = jnp.where(alive_mask, pix_ids + 1, 0).astype(jnp.float32)
    all_rows, all_tags = side_by_side((shade_rows, tagged), "gauss", 0, 1)
    own_tags = jnp.where(alive_mask, pix_ids + 1, -1).astype(jnp.float32)
    match_hot = (own_tags[:, None] == all_tags[None, :]).astype(jnp.float32)
    jp_rows = jnp.dot(match_hot, all_rows, precision=lax.Precision.HIGHEST)
    jp_round = jp_rows.astype(jnp.bfloat16)
    curv_terms = jnp.einsum("tpgx,tx->tpg", tiles_now, jp_round, preferred_element_type=jnp.float32)
    curv_acc = jnp.sum(block_hot.T[:, :, None, None] * curv_terms[None], axis=1)
    resid_rows = jnp.take(residual[0], pix_ids, axis=0)
    grad_terms = jnp.einsum(
        "tpgx,tx->tpg", tiles_now, resid_rows, preferred_element_type=jnp.float32
    )
    grad_acc = jnp.sum(block_hot.T[:, :, None, None] * grad_terms[None], axis=1)
    both_sum = over_copies(jnp.stack([grad_acc, curv_acc]), "view")
    return (both_sum[0], both_sum[1], gram_sum)


def solution(mesh):
    placed = (
        P("view", "gauss", None, None, None),
        P("view", "gauss"),
        P("view", "gauss"),
        P("view", "gauss"),
        P("view", None, None),
        P("gauss", None, None),
    )
    return jax.shard_map(
        local,
        mesh=mesh,
        in_specs=placed,
        out_specs=(P("gauss", None, None), P("gauss", None, None), P("gauss", None, None, None)),
        check_vma=False,
    )
```

```python
import math

import jax
import jax.numpy as jnp
import numpy as np
from jax import lax
from jax.sharding import PartitionSpec as P
from jax.experimental import pallas as pl
from jax.experimental.pallas import tpu as pltpu


def side_by_side(arrays, axis, dim, along):
    widths = [math.prod(a.shape[along:]) for a in arrays]
    both = jnp.concatenate(
        [a.reshape(*a.shape[:along], w) for a, w in zip(arrays, widths)], axis=along
    )
    result = copy_for_each(both, axis).reshape(-1, *both.shape[1:])
    blocks = jnp.split(result, [sum(widths[:k]) for k in range(1, len(widths))], axis=along)
    return tuple(
        (b.reshape(*result.shape[:along], *a.shape[along:]) for a, b in zip(arrays, blocks))
    )


def copy_for_each(array, axis):
    length = lax.axis_size(axis)
    return lax.all_to_all(
        jnp.broadcast_to(array[None], (length, *array.shape)), axis, 0, 0, tiled=True
    )


def over_copies(array, axis):
    everything = copy_for_each(array, axis)
    return jnp.sum(everything, axis=0)


P_PAD = 64
GROUP = 4


def row_offsets(size):
    return [p * size - p * (p - 1) // 2 for p in range(size)]


def gram_kernel(w_ref, jac_ref, out_ref, xf_ref, sc_ref, acc_ref):
    t = pl.program_id(0)
    size = jac_ref.shape[0]
    gb = jac_ref.shape[1]
    nb = acc_ref.shape[0]
    halves = xf_ref.shape[0]
    span = P_PAD * 8

    @pl.when(t == 0)
    def _init():
        for h in range(halves):
            for c in range(gb // 8):
                xf_ref[h, pl.ds(c * span + size * 8, (P_PAD - size) * 8), :] = jnp.zeros(((P_PAD - size) * 8, 128), jnp.float32)
        acc_ref[...] = jnp.zeros(acc_ref.shape, jnp.float32)

    for p in range(size):
        for h in range(halves):
            slab = jac_ref[p, :, h * 128:(h + 1) * 128].astype(jnp.float32)
            for c in range(gb // 8):
                xf_ref[h, pl.ds(c * span + p * 8, 8), :] = slab[c * 8:(c + 1) * 8]

    for c in range(gb // GROUP):
        parts = []
        for i in range(GROUP):
            g = c * GROUP + i
            base = (g // 8) * span + g % 8
            parts.append(jnp.concatenate([xf_ref[h, pl.ds(base, P_PAD, stride=8), :] for h in range(halves)], axis=1))
        a = jnp.concatenate(parts, axis=0).astype(jnp.bfloat16)
        prod = lax.dot_general(a, a, (((1,), (1,)), ((), ())), preferred_element_type=jnp.float32)
        for i in range(GROUP):
            g = c * GROUP + i
            lane0 = 128 * ((i * P_PAD) // 128)
            block = prod[i * P_PAD:(i + 1) * P_PAD, lane0:lane0 + 128]
            for r in range(P_PAD // 8):
                sc_ref[pl.ds(r * gb * 8 + g * 8, 8), :] = block[r * 8:(r + 1) * 8]

    odd = (lax.broadcasted_iota(jnp.int32, (P_PAD, gb), 1) % 2) == 1
    weights = [w_ref[t, b] for b in range(nb)]
    for p in range(size):
        s = sc_ref[pl.ds((p // 8) * gb * 8 + p % 8, gb, stride=8), :]
        tr = s.T
        row = jnp.where(odd, tr[P_PAD:2 * P_PAD], tr[0:P_PAD])
        for b in range(nb):
            acc_ref[b, p] += weights[b] * row

    @pl.when(t == pl.num_programs(0) - 1)
    def _pack():
        offs = row_offsets(size)
        for b in range(nb):
            for p in range(size):
                out_ref[b, pl.ds(offs[p], size - p), :] = acc_ref[b, p, pl.ds(p, size - p), :]


def gram_packed(tiles, weights):
    nt, size, gb, nx = tiles.shape
    nb = weights.shape[1]
    packed_rows = size * (size + 1) // 2
    return pl.pallas_call(
        gram_kernel,
        grid=(nt,),
        in_specs=[
            pl.BlockSpec(memory_space=pltpu.SMEM),
            pl.BlockSpec((None, size, gb, nx), lambda t: (t, 0, 0, 0)),
        ],
        out_specs=pl.BlockSpec((nb, packed_rows, gb), lambda t: (0, 0, 0)),
        out_shape=jax.ShapeDtypeStruct((nb, packed_rows, gb), jnp.float32),
        scratch_shapes=[
            pltpu.VMEM((nx // 128, P_PAD * gb, 128), jnp.float32),
            pltpu.VMEM((gb * P_PAD, 128), jnp.float32),
            pltpu.VMEM((nb, size, P_PAD, gb), jnp.float32),
        ],
        compiler_params=pltpu.CompilerParams(vmem_limit_bytes=48 * 1024 * 1024),
    )(weights, tiles)


ROW_CHUNK = 8


def unpack_kernel(packed_ref, out_ref, u_ref):
    step = pl.program_id(0)
    size, nb = out_ref.shape[1], out_ref.shape[2]
    offs = row_offsets(size)
    q_id = lax.broadcasted_iota(jnp.int32, (P_PAD, out_ref.shape[3]), 0)

    @pl.when(step == 0)
    def _fill():
        for b in range(nb):
            for p in range(size):
                u_ref[b, pl.ds(p * P_PAD + p, size - p), :] = packed_ref[b, pl.ds(offs[p], size - p), :]

    for c in range(pl.cdiv(size, ROW_CHUNK)):
        @pl.when(step == c)
        def _rows():
            for p in range(c * ROW_CHUNK, min(size, (c + 1) * ROW_CHUNK)):
                rows = []
                for b in range(nb):
                    up = u_ref[b, pl.ds(p * P_PAD, P_PAD), :]
                    low = u_ref[b, pl.ds(p, P_PAD, stride=P_PAD), :]
                    rows.append(jnp.where(q_id >= p, up, low)[0:size])
                out_ref[p - c * ROW_CHUNK] = jnp.stack(rows, axis=1)


def unpack(packed, size):
    nb, rows, gb = packed.shape
    full = pl.pallas_call(
        unpack_kernel,
        grid=(pl.cdiv(size, ROW_CHUNK),),
        in_specs=[pl.BlockSpec((nb, rows, gb), lambda i: (0, 0, 0))],
        out_specs=pl.BlockSpec((ROW_CHUNK, size, nb, gb), lambda i: (i, 0, 0, 0)),
        out_shape=jax.ShapeDtypeStruct((size, size, nb, gb), jnp.float32),
        scratch_shapes=[pltpu.VMEM((nb, P_PAD * P_PAD, gb), jnp.float32)],
    )(packed)
    return jnp.transpose(full, (2, 0, 1, 3))


def local(jac, tile_count, tile_block, tile_pix, residual, direction):
    slot_total = jac.shape[1]
    blocks = direction.shape[0]
    size = jac.shape[2]
    live_count = tile_count[0, 0]
    block_ids = tile_block[0]
    pix_ids = tile_pix[0]
    alive_mask = jnp.arange(slot_total) < live_count
    alive_float = alive_mask.astype(jnp.float32)
    tiles_now = jac[0]
    block_match = block_ids[:, None] == jnp.arange(blocks)[None, :]
    block_hot = (block_match & alive_mask[:, None]).astype(jnp.float32)

    packed_gram = gram_packed(tiles_now, block_hot)
    packed_gram, tiles_now = lax.optimization_barrier((packed_gram, tiles_now))
    summed = lax.psum(packed_gram, "view")
    gram_sum = unpack(summed, size)

    dir_rows = jnp.take(direction, block_ids, axis=0)
    shade_rows = (
        jnp.einsum("tpgx,tpg->tx", tiles_now, dir_rows, preferred_element_type=jnp.float32)
        * alive_float[:, None]
    )
    tagged = jnp.where(alive_mask, pix_ids + 1, 0).astype(jnp.float32)
    all_rows, all_tags = side_by_side((shade_rows, tagged), "gauss", 0, 1)
    own_tags = jnp.where(alive_mask, pix_ids + 1, -1).astype(jnp.float32)
    match_hot = (own_tags[:, None] == all_tags[None, :]).astype(jnp.float32)
    jp_rows = jnp.dot(match_hot, all_rows, precision=lax.Precision.HIGHEST)
    jp_round = jp_rows.astype(jnp.bfloat16)
    curv_terms = jnp.einsum("tpgx,tx->tpg", tiles_now, jp_round, preferred_element_type=jnp.float32)
    curv_acc = jnp.sum(block_hot.T[:, :, None, None] * curv_terms[None], axis=1)
    resid_rows = jnp.take(residual[0], pix_ids, axis=0)
    grad_terms = jnp.einsum(
        "tpgx,tx->tpg", tiles_now, resid_rows, preferred_element_type=jnp.float32
    )
    grad_acc = jnp.sum(block_hot.T[:, :, None, None] * grad_terms[None], axis=1)
    both_sum = over_copies(jnp.stack([grad_acc, curv_acc]), "view")
    return (both_sum[0], both_sum[1], gram_sum)


def solution(mesh):
    placed = (
        P("view", "gauss", None, None, None),
        P("view", "gauss"),
        P("view", "gauss"),
        P("view", "gauss"),
        P("view", None, None),
        P("gauss", None, None),
    )
    return jax.shard_map(
        local,
        mesh=mesh,
        in_specs=placed,
        out_specs=(P("gauss", None, None), P("gauss", None, None), P("gauss", None, None, None)),
        check_vma=False,
    )
```

```python
import math

import jax
import jax.numpy as jnp
import numpy as np
from jax import lax
from jax.sharding import PartitionSpec as P
from jax.experimental import pallas as pl
from jax.experimental.pallas import tpu as pltpu


def side_by_side(arrays, axis, dim, along):
    widths = [math.prod(a.shape[along:]) for a in arrays]
    both = jnp.concatenate(
        [a.reshape(*a.shape[:along], w) for a, w in zip(arrays, widths)], axis=along
    )
    result = copy_for_each(both, axis).reshape(-1, *both.shape[1:])
    blocks = jnp.split(result, [sum(widths[:k]) for k in range(1, len(widths))], axis=along)
    return tuple(
        (b.reshape(*result.shape[:along], *a.shape[along:]) for a, b in zip(arrays, blocks))
    )


def copy_for_each(array, axis):
    length = lax.axis_size(axis)
    return lax.all_to_all(
        jnp.broadcast_to(array[None], (length, *array.shape)), axis, 0, 0, tiled=True
    )


def over_copies(array, axis):
    everything = copy_for_each(array, axis)
    return jnp.sum(everything, axis=0)


P_PAD = 64
GROUP = 4


def row_offsets(size):
    return [p * size - p * (p - 1) // 2 for p in range(size)]


def gram_kernel(w_ref, jac_ref, out_ref, xf_ref, sc_ref, acc_ref):
    t = pl.program_id(0)
    size = jac_ref.shape[0]
    gb = jac_ref.shape[1]
    nb = acc_ref.shape[0]
    halves = xf_ref.shape[0]
    span = P_PAD * 8

    @pl.when(t == 0)
    def _init():
        for h in range(halves):
            for c in range(gb // 8):
                xf_ref[h, pl.ds(c * span + size * 8, (P_PAD - size) * 8), :] = jnp.zeros(((P_PAD - size) * 8, 128), jnp.float32)
        acc_ref[...] = jnp.zeros(acc_ref.shape, jnp.float32)

    for p in range(size):
        for h in range(halves):
            slab = jac_ref[p, :, h * 128:(h + 1) * 128].astype(jnp.float32)
            for c in range(gb // 8):
                xf_ref[h, pl.ds(c * span + p * 8, 8), :] = slab[c * 8:(c + 1) * 8]

    for c in range(gb // GROUP):
        parts = []
        for i in range(GROUP):
            g = c * GROUP + i
            base = (g // 8) * span + g % 8
            parts.append(jnp.concatenate([xf_ref[h, pl.ds(base, P_PAD, stride=8), :] for h in range(halves)], axis=1))
        a = jnp.concatenate(parts, axis=0).astype(jnp.bfloat16)
        prod = lax.dot_general(a, a, (((1,), (1,)), ((), ())), preferred_element_type=jnp.float32)
        for i in range(GROUP):
            g = c * GROUP + i
            lane0 = 128 * ((i * P_PAD) // 128)
            block = prod[i * P_PAD:(i + 1) * P_PAD, lane0:lane0 + 128]
            for r in range(P_PAD // 8):
                sc_ref[pl.ds(r * gb * 8 + g * 8, 8), :] = block[r * 8:(r + 1) * 8]

    odd = (lax.broadcasted_iota(jnp.int32, (P_PAD, gb), 1) % 2) == 1
    weights = [w_ref[t, b] for b in range(nb)]
    for p in range(size):
        s = sc_ref[pl.ds((p // 8) * gb * 8 + p % 8, gb, stride=8), :]
        tr = s.T
        row = jnp.where(odd, tr[P_PAD:2 * P_PAD], tr[0:P_PAD])
        for b in range(nb):
            acc_ref[b, p] += weights[b] * row

    @pl.when(t == pl.num_programs(0) - 1)
    def _pack():
        offs = row_offsets(size)
        for b in range(nb):
            for p in range(size):
                out_ref[b, pl.ds(offs[p], size - p), :] = acc_ref[b, p, pl.ds(p, size - p), :]


def gram_packed(tiles, weights):
    nt, size, gb, nx = tiles.shape
    nb = weights.shape[1]
    packed_rows = size * (size + 1) // 2
    return pl.pallas_call(
        gram_kernel,
        grid=(nt,),
        in_specs=[
            pl.BlockSpec(memory_space=pltpu.SMEM),
            pl.BlockSpec((None, size, gb, nx), lambda t: (t, 0, 0, 0)),
        ],
        out_specs=pl.BlockSpec((nb, packed_rows, gb), lambda t: (0, 0, 0)),
        out_shape=jax.ShapeDtypeStruct((nb, packed_rows, gb), jnp.float32),
        scratch_shapes=[
            pltpu.VMEM((nx // 128, P_PAD * gb, 128), jnp.float32),
            pltpu.VMEM((gb * P_PAD, 128), jnp.float32),
            pltpu.VMEM((nb, size, P_PAD, gb), jnp.float32),
        ],
        compiler_params=pltpu.CompilerParams(vmem_limit_bytes=48 * 1024 * 1024),
    )(weights, tiles)


ROW_CHUNK = 8


def unpack_kernel(packed_ref, out_ref, u_ref):
    step = pl.program_id(0)
    size, nb = out_ref.shape[1], out_ref.shape[2]
    offs = row_offsets(size)
    span = P_PAD * 8
    q_id = lax.broadcasted_iota(jnp.int32, (P_PAD, out_ref.shape[3]), 0)

    @pl.when(step == 0)
    def _fill():
        for b in range(nb):
            for p in range(size):
                for qb in range(p // 8, pl.cdiv(size, 8)):
                    q0 = max(p, qb * 8)
                    q1 = min(size, qb * 8 + 8)
                    u_ref[b, pl.ds(qb * span + p * 8 + q0 % 8, q1 - q0), :] = packed_ref[b, pl.ds(offs[p] + q0 - p, q1 - q0), :]

    for c in range(pl.cdiv(size, ROW_CHUNK)):
        @pl.when(step == c)
        def _rows():
            for p in range(c * ROW_CHUNK, min(size, (c + 1) * ROW_CHUNK)):
                rows = []
                for b in range(nb):
                    up = jnp.concatenate([u_ref[b, pl.ds(qb * span + p * 8, 8), :] for qb in range(P_PAD // 8)], axis=0)
                    low = u_ref[b, pl.ds((p // 8) * span + p % 8, P_PAD, stride=8), :]
                    rows.append(jnp.where(q_id >= p, up, low)[0:size])
                out_ref[p - c * ROW_CHUNK] = jnp.stack(rows, axis=1)


def unpack(packed, size):
    nb, rows, gb = packed.shape
    full = pl.pallas_call(
        unpack_kernel,
        grid=(pl.cdiv(size, ROW_CHUNK),),
        in_specs=[pl.BlockSpec((nb, rows, gb), lambda i: (0, 0, 0))],
        out_specs=pl.BlockSpec((ROW_CHUNK, size, nb, gb), lambda i: (i, 0, 0, 0)),
        out_shape=jax.ShapeDtypeStruct((size, size, nb, gb), jnp.float32),
        scratch_shapes=[pltpu.VMEM((nb, P_PAD * P_PAD, gb), jnp.float32)],
    )(packed)
    return jnp.transpose(full, (2, 0, 1, 3))


def local(jac, tile_count, tile_block, tile_pix, residual, direction):
    slot_total = jac.shape[1]
    blocks = direction.shape[0]
    size = jac.shape[2]
    live_count = tile_count[0, 0]
    block_ids = tile_block[0]
    pix_ids = tile_pix[0]
    alive_mask = jnp.arange(slot_total) < live_count
    alive_float = alive_mask.astype(jnp.float32)
    tiles_now = jac[0]
    block_match = block_ids[:, None] == jnp.arange(blocks)[None, :]
    block_hot = (block_match & alive_mask[:, None]).astype(jnp.float32)

    packed_gram = gram_packed(tiles_now, block_hot)
    packed_gram, tiles_now = lax.optimization_barrier((packed_gram, tiles_now))
    summed = lax.psum(packed_gram, "view")
    gram_sum = unpack(summed, size)

    dir_rows = jnp.take(direction, block_ids, axis=0)
    shade_rows = (
        jnp.einsum("tpgx,tpg->tx", tiles_now, dir_rows, preferred_element_type=jnp.float32)
        * alive_float[:, None]
    )
    tagged = jnp.where(alive_mask, pix_ids + 1, 0).astype(jnp.float32)
    all_rows, all_tags = side_by_side((shade_rows, tagged), "gauss", 0, 1)
    own_tags = jnp.where(alive_mask, pix_ids + 1, -1).astype(jnp.float32)
    match_hot = (own_tags[:, None] == all_tags[None, :]).astype(jnp.float32)
    jp_rows = jnp.dot(match_hot, all_rows, precision=lax.Precision.HIGHEST)
    jp_round = jp_rows.astype(jnp.bfloat16)
    curv_terms = jnp.einsum("tpgx,tx->tpg", tiles_now, jp_round, preferred_element_type=jnp.float32)
    curv_acc = jnp.sum(block_hot.T[:, :, None, None] * curv_terms[None], axis=1)
    resid_rows = jnp.take(residual[0], pix_ids, axis=0)
    grad_terms = jnp.einsum(
        "tpgx,tx->tpg", tiles_now, resid_rows, preferred_element_type=jnp.float32
    )
    grad_acc = jnp.sum(block_hot.T[:, :, None, None] * grad_terms[None], axis=1)
    both_sum = over_copies(jnp.stack([grad_acc, curv_acc]), "view")
    return (both_sum[0], both_sum[1], gram_sum)


def solution(mesh):
    placed = (
        P("view", "gauss", None, None, None),
        P("view", "gauss"),
        P("view", "gauss"),
        P("view", "gauss"),
        P("view", None, None),
        P("gauss", None, None),
    )
    return jax.shard_map(
        local,
        mesh=mesh,
        in_specs=placed,
        out_specs=(P("gauss", None, None), P("gauss", None, None), P("gauss", None, None, None)),
        check_vma=False,
    )
```

```python
import math

import jax
import jax.numpy as jnp
import numpy as np
from jax import lax
from jax.sharding import PartitionSpec as P
from jax.experimental import pallas as pl
from jax.experimental.pallas import tpu as pltpu


def side_by_side(arrays, axis, dim, along):
    widths = [math.prod(a.shape[along:]) for a in arrays]
    both = jnp.concatenate(
        [a.reshape(*a.shape[:along], w) for a, w in zip(arrays, widths)], axis=along
    )
    result = copy_for_each(both, axis).reshape(-1, *both.shape[1:])
    blocks = jnp.split(result, [sum(widths[:k]) for k in range(1, len(widths))], axis=along)
    return tuple(
        (b.reshape(*result.shape[:along], *a.shape[along:]) for a, b in zip(arrays, blocks))
    )


def copy_for_each(array, axis):
    length = lax.axis_size(axis)
    return lax.all_to_all(
        jnp.broadcast_to(array[None], (length, *array.shape)), axis, 0, 0, tiled=True
    )


def over_copies(array, axis):
    everything = copy_for_each(array, axis)
    return jnp.sum(everything, axis=0)


P_PAD = 64
GROUP = 4


def row_offsets(size):
    return [p * size - p * (p - 1) // 2 for p in range(size)]


def gram_kernel(w_ref, jac_ref, out_ref, xf_ref, sc_ref, acc_ref):
    t = pl.program_id(0)
    size = jac_ref.shape[0]
    gb = jac_ref.shape[1]
    nb = acc_ref.shape[0]
    halves = xf_ref.shape[0]
    span = P_PAD * 8

    @pl.when(t == 0)
    def _init():
        for h in range(halves):
            for c in range(gb // 8):
                xf_ref[h, pl.ds(c * span + size * 8, (P_PAD - size) * 8), :] = jnp.zeros(((P_PAD - size) * 8, 128), jnp.float32)
        acc_ref[...] = jnp.zeros(acc_ref.shape, jnp.float32)

    for p in range(size):
        for h in range(halves):
            slab = jac_ref[p, :, h * 128:(h + 1) * 128].astype(jnp.float32)
            for c in range(gb // 8):
                xf_ref[h, pl.ds(c * span + p * 8, 8), :] = slab[c * 8:(c + 1) * 8]

    for c in range(gb // GROUP):
        parts = []
        for i in range(GROUP):
            g = c * GROUP + i
            base = (g // 8) * span + g % 8
            parts.append(jnp.concatenate([xf_ref[h, pl.ds(base, P_PAD, stride=8), :] for h in range(halves)], axis=1))
        a = jnp.concatenate(parts, axis=0).astype(jnp.bfloat16)
        prod = lax.dot_general(a, a, (((1,), (1,)), ((), ())), preferred_element_type=jnp.float32)
        for i in range(GROUP):
            g = c * GROUP + i
            lane0 = 128 * ((i * P_PAD) // 128)
            block = prod[i * P_PAD:(i + 1) * P_PAD, lane0:lane0 + 128]
            for r in range(P_PAD // 8):
                sc_ref[pl.ds(r * gb * 8 + g * 8, 8), :] = block[r * 8:(r + 1) * 8]

    odd = (lax.broadcasted_iota(jnp.int32, (P_PAD, gb), 1) % 2) == 1
    weights = [w_ref[t, b] for b in range(nb)]
    for p in range(size):
        s = sc_ref[pl.ds((p // 8) * gb * 8 + p % 8, gb, stride=8), :]
        tr = s.T
        row = jnp.where(odd, tr[P_PAD:2 * P_PAD], tr[0:P_PAD])
        for b in range(nb):
            acc_ref[b, p] += weights[b] * row

    @pl.when(t == pl.num_programs(0) - 1)
    def _pack():
        offs = row_offsets(size)
        tail = out_ref.shape[1] - size * (size + 1) // 2
        for b in range(nb):
            out_ref[b, pl.ds(out_ref.shape[1] - tail, tail), :] = jnp.zeros((tail, out_ref.shape[2]), jnp.float32)
            for p in range(size):
                out_ref[b, pl.ds(offs[p], size - p), :] = acc_ref[b, p, pl.ds(p, size - p), :]


def gram_packed(tiles, weights):
    nt, size, gb, nx = tiles.shape
    nb = weights.shape[1]
    packed_rows = -(-(size * (size + 1) // 2) // 8) * 8
    return pl.pallas_call(
        gram_kernel,
        grid=(nt,),
        in_specs=[
            pl.BlockSpec(memory_space=pltpu.SMEM),
            pl.BlockSpec((None, size, gb, nx), lambda t: (t, 0, 0, 0)),
        ],
        out_specs=pl.BlockSpec((nb, packed_rows, gb), lambda t: (0, 0, 0)),
        out_shape=jax.ShapeDtypeStruct((nb, packed_rows, gb), jnp.float32),
        scratch_shapes=[
            pltpu.VMEM((nx // 128, P_PAD * gb, 128), jnp.float32),
            pltpu.VMEM((gb * P_PAD, 128), jnp.float32),
            pltpu.VMEM((nb, size, P_PAD, gb), jnp.float32),
        ],
        compiler_params=pltpu.CompilerParams(vmem_limit_bytes=48 * 1024 * 1024),
    )(weights, tiles)


ROW_CHUNK = 8


def unpack_kernel(packed_ref, out_ref, u_ref):
    step = pl.program_id(0)
    size, nb = out_ref.shape[1], out_ref.shape[2]
    offs = row_offsets(size)
    span = P_PAD * 8
    q_id = lax.broadcasted_iota(jnp.int32, (P_PAD, out_ref.shape[3]), 0)

    @pl.when(step == 0)
    def _fill():
        for b in range(nb):
            for p in range(size):
                for qb in range(p // 8, pl.cdiv(size, 8)):
                    q0 = max(p, qb * 8)
                    q1 = min(size, qb * 8 + 8)
                    u_ref[b, pl.ds(qb * span + p * 8 + q0 % 8, q1 - q0), :] = packed_ref[b, pl.ds(offs[p] + q0 - p, q1 - q0), :]

    for c in range(pl.cdiv(size, ROW_CHUNK)):
        @pl.when(step == c)
        def _rows():
            for p in range(c * ROW_CHUNK, min(size, (c + 1) * ROW_CHUNK)):
                rows = []
                for b in range(nb):
                    up = jnp.concatenate([u_ref[b, pl.ds(qb * span + p * 8, 8), :] for qb in range(P_PAD // 8)], axis=0)
                    low = u_ref[b, pl.ds((p // 8) * span + p % 8, P_PAD, stride=8), :]
                    rows.append(jnp.where(q_id >= p, up, low)[0:size])
                out_ref[p - c * ROW_CHUNK] = jnp.stack(rows, axis=1)


def unpack(packed, size):
    nb, rows, gb = packed.shape
    full = pl.pallas_call(
        unpack_kernel,
        grid=(pl.cdiv(size, ROW_CHUNK),),
        in_specs=[pl.BlockSpec((nb, rows, gb), lambda i: (0, 0, 0))],
        out_specs=pl.BlockSpec((ROW_CHUNK, size, nb, gb), lambda i: (i, 0, 0, 0)),
        out_shape=jax.ShapeDtypeStruct((size, size, nb, gb), jnp.float32),
        scratch_shapes=[pltpu.VMEM((nb, P_PAD * P_PAD, gb), jnp.float32)],
    )(packed)
    return jnp.transpose(full, (2, 0, 1, 3))


def local(jac, tile_count, tile_block, tile_pix, residual, direction):
    slot_total = jac.shape[1]
    blocks = direction.shape[0]
    size = jac.shape[2]
    live_count = tile_count[0, 0]
    block_ids = tile_block[0]
    pix_ids = tile_pix[0]
    alive_mask = jnp.arange(slot_total) < live_count
    alive_float = alive_mask.astype(jnp.float32)
    tiles_now = jac[0]
    block_match = block_ids[:, None] == jnp.arange(blocks)[None, :]
    block_hot = (block_match & alive_mask[:, None]).astype(jnp.float32)

    packed_gram = gram_packed(tiles_now, block_hot)
    packed_gram, tiles_now = lax.optimization_barrier((packed_gram, tiles_now))
    parts = lax.axis_size("view")
    chunks = packed_gram.reshape(parts, -1, packed_gram.shape[2])
    mine = jnp.sum(lax.all_to_all(chunks, "view", 0, 0, tiled=True), axis=0)
    summed = copy_for_each(mine, "view").reshape(packed_gram.shape)
    gram_sum = unpack(summed, size)

    dir_rows = jnp.take(direction, block_ids, axis=0)
    shade_rows = (
        jnp.einsum("tpgx,tpg->tx", tiles_now, dir_rows, preferred_element_type=jnp.float32)
        * alive_float[:, None]
    )
    tagged = jnp.where(alive_mask, pix_ids + 1, 0).astype(jnp.float32)
    all_rows, all_tags = side_by_side((shade_rows, tagged), "gauss", 0, 1)
    own_tags = jnp.where(alive_mask, pix_ids + 1, -1).astype(jnp.float32)
    match_hot = (own_tags[:, None] == all_tags[None, :]).astype(jnp.float32)
    jp_rows = jnp.dot(match_hot, all_rows, precision=lax.Precision.HIGHEST)
    jp_round = jp_rows.astype(jnp.bfloat16)
    curv_terms = jnp.einsum("tpgx,tx->tpg", tiles_now, jp_round, preferred_element_type=jnp.float32)
    curv_acc = jnp.sum(block_hot.T[:, :, None, None] * curv_terms[None], axis=1)
    resid_rows = jnp.take(residual[0], pix_ids, axis=0)
    grad_terms = jnp.einsum(
        "tpgx,tx->tpg", tiles_now, resid_rows, preferred_element_type=jnp.float32
    )
    grad_acc = jnp.sum(block_hot.T[:, :, None, None] * grad_terms[None], axis=1)
    both_sum = over_copies(jnp.stack([grad_acc, curv_acc]), "view")
    return (both_sum[0], both_sum[1], gram_sum)


def solution(mesh):
    placed = (
        P("view", "gauss", None, None, None),
        P("view", "gauss"),
        P("view", "gauss"),
        P("view", "gauss"),
        P("view", None, None),
        P("gauss", None, None),
    )
    return jax.shard_map(
        local,
        mesh=mesh,
        in_specs=placed,
        out_specs=(P("gauss", None, None), P("gauss", None, None), P("gauss", None, None, None)),
        check_vma=False,
    )
```

```python
import math

import jax
import jax.numpy as jnp
import numpy as np
from jax import lax
from jax.sharding import PartitionSpec as P
from jax.experimental import pallas as pl
from jax.experimental.pallas import tpu as pltpu


def side_by_side(arrays, axis, dim, along):
    widths = [math.prod(a.shape[along:]) for a in arrays]
    both = jnp.concatenate(
        [a.reshape(*a.shape[:along], w) for a, w in zip(arrays, widths)], axis=along
    )
    result = copy_for_each(both, axis).reshape(-1, *both.shape[1:])
    blocks = jnp.split(result, [sum(widths[:k]) for k in range(1, len(widths))], axis=along)
    return tuple(
        (b.reshape(*result.shape[:along], *a.shape[along:]) for a, b in zip(arrays, blocks))
    )


def copy_for_each(array, axis):
    length = lax.axis_size(axis)
    return lax.all_to_all(
        jnp.broadcast_to(array[None], (length, *array.shape)), axis, 0, 0, tiled=True
    )


def over_copies(array, axis):
    everything = copy_for_each(array, axis)
    return jnp.sum(everything, axis=0)


P_PAD = 64
GROUP = 2


def row_offsets(size):
    return [p * size - p * (p - 1) // 2 for p in range(size)]


def gram_kernel(w_ref, jac_ref, out_ref, xf_ref, sc_ref, acc_ref):
    t = pl.program_id(0)
    size = jac_ref.shape[0]
    gb = jac_ref.shape[1]
    nb = acc_ref.shape[0]
    halves = xf_ref.shape[0]
    span = P_PAD * 8

    @pl.when(t == 0)
    def _init():
        for h in range(halves):
            for c in range(gb // 8):
                xf_ref[h, pl.ds(c * span + size * 8, (P_PAD - size) * 8), :] = jnp.zeros(((P_PAD - size) * 8, 128), jnp.float32)
        acc_ref[...] = jnp.zeros(acc_ref.shape, jnp.float32)

    for p in range(size):
        for h in range(halves):
            slab = jac_ref[p, :, h * 128:(h + 1) * 128].astype(jnp.float32)
            for c in range(gb // 8):
                xf_ref[h, pl.ds(c * span + p * 8, 8), :] = slab[c * 8:(c + 1) * 8]

    for c in range(gb // GROUP):
        parts = []
        for i in range(GROUP):
            g = c * GROUP + i
            base = (g // 8) * span + g % 8
            parts.append(jnp.concatenate([xf_ref[h, pl.ds(base, P_PAD, stride=8), :] for h in range(halves)], axis=1))
        a = jnp.concatenate(parts, axis=0).astype(jnp.bfloat16)
        prod = lax.dot_general(a, a, (((1,), (1,)), ((), ())), preferred_element_type=jnp.float32)
        for i in range(GROUP):
            g = c * GROUP + i
            lane0 = 128 * ((i * P_PAD) // 128)
            block = prod[i * P_PAD:(i + 1) * P_PAD, lane0:lane0 + 128]
            for r in range(P_PAD // 8):
                sc_ref[pl.ds(r * gb * 8 + g * 8, 8), :] = block[r * 8:(r + 1) * 8]

    odd = (lax.broadcasted_iota(jnp.int32, (P_PAD, gb), 1) % 2) == 1
    alive = w_ref[t, 0]
    blk = jnp.int32(0)
    for b in range(1, nb):
        alive = alive + w_ref[t, b]
        blk = jnp.where(w_ref[t, b] > 0, jnp.int32(b), blk)
    for p in range(size):
        s = sc_ref[pl.ds((p // 8) * gb * 8 + p % 8, gb, stride=8), :]
        tr = s.T
        row = jnp.where(odd, tr[P_PAD:2 * P_PAD], tr[0:P_PAD])
        acc_ref[blk, p] += alive * row

    @pl.when(t == pl.num_programs(0) - 1)
    def _pack():
        offs = row_offsets(size)
        for b in range(nb):
            for p in range(size):
                out_ref[b, pl.ds(offs[p], size - p), :] = acc_ref[b, p, pl.ds(p, size - p), :]


def gram_packed(tiles, weights):
    nt, size, gb, nx = tiles.shape
    nb = weights.shape[1]
    packed_rows = size * (size + 1) // 2
    return pl.pallas_call(
        gram_kernel,
        grid=(nt,),
        in_specs=[
            pl.BlockSpec(memory_space=pltpu.SMEM),
            pl.BlockSpec((None, size, gb, nx), lambda t: (t, 0, 0, 0)),
        ],
        out_specs=pl.BlockSpec((nb, packed_rows, gb), lambda t: (0, 0, 0)),
        out_shape=jax.ShapeDtypeStruct((nb, packed_rows, gb), jnp.float32),
        scratch_shapes=[
            pltpu.VMEM((nx // 128, P_PAD * gb, 128), jnp.float32),
            pltpu.VMEM((gb * P_PAD, 128), jnp.float32),
            pltpu.VMEM((nb, size, P_PAD, gb), jnp.float32),
        ],
        compiler_params=pltpu.CompilerParams(vmem_limit_bytes=48 * 1024 * 1024),
    )(weights, tiles)


ROW_CHUNK = 8


def unpack_kernel(packed_ref, out_ref, u_ref):
    step = pl.program_id(0)
    size, nb = out_ref.shape[1], out_ref.shape[2]
    offs = row_offsets(size)
    span = P_PAD * 8
    q_id = lax.broadcasted_iota(jnp.int32, (P_PAD, out_ref.shape[3]), 0)

    @pl.when(step == 0)
    def _fill():
        for b in range(nb):
            for p in range(size):
                for qb in range(p // 8, pl.cdiv(size, 8)):
                    q0 = max(p, qb * 8)
                    q1 = min(size, qb * 8 + 8)
                    u_ref[b, pl.ds(qb * span + p * 8 + q0 % 8, q1 - q0), :] = packed_ref[b, pl.ds(offs[p] + q0 - p, q1 - q0), :]

    for c in range(pl.cdiv(size, ROW_CHUNK)):
        @pl.when(step == c)
        def _rows():
            for p in range(c * ROW_CHUNK, min(size, (c + 1) * ROW_CHUNK)):
                rows = []
                for b in range(nb):
                    up = jnp.concatenate([u_ref[b, pl.ds(qb * span + p * 8, 8), :] for qb in range(P_PAD // 8)], axis=0)
                    low = u_ref[b, pl.ds((p // 8) * span + p % 8, P_PAD, stride=8), :]
                    rows.append(jnp.where(q_id >= p, up, low)[0:size])
                out_ref[p - c * ROW_CHUNK] = jnp.stack(rows, axis=1)


def unpack(packed, size):
    nb, rows, gb = packed.shape
    full = pl.pallas_call(
        unpack_kernel,
        grid=(pl.cdiv(size, ROW_CHUNK),),
        in_specs=[pl.BlockSpec((nb, rows, gb), lambda i: (0, 0, 0))],
        out_specs=pl.BlockSpec((ROW_CHUNK, size, nb, gb), lambda i: (i, 0, 0, 0)),
        out_shape=jax.ShapeDtypeStruct((size, size, nb, gb), jnp.float32),
        scratch_shapes=[pltpu.VMEM((nb, P_PAD * P_PAD, gb), jnp.float32)],
    )(packed)
    return jnp.transpose(full, (2, 0, 1, 3))


def local(jac, tile_count, tile_block, tile_pix, residual, direction):
    slot_total = jac.shape[1]
    blocks = direction.shape[0]
    size = jac.shape[2]
    live_count = tile_count[0, 0]
    block_ids = tile_block[0]
    pix_ids = tile_pix[0]
    alive_mask = jnp.arange(slot_total) < live_count
    alive_float = alive_mask.astype(jnp.float32)
    tiles_now = jac[0]
    block_match = block_ids[:, None] == jnp.arange(blocks)[None, :]
    block_hot = (block_match & alive_mask[:, None]).astype(jnp.float32)

    packed_gram = gram_packed(tiles_now, block_hot)
    packed_gram, tiles_now = lax.optimization_barrier((packed_gram, tiles_now))
    summed = lax.psum(packed_gram, "view")
    gram_sum = unpack(summed, size)

    dir_rows = jnp.take(direction, block_ids, axis=0)
    shade_rows = (
        jnp.einsum("tpgx,tpg->tx", tiles_now, dir_rows, preferred_element_type=jnp.float32)
        * alive_float[:, None]
    )
    tagged = jnp.where(alive_mask, pix_ids + 1, 0).astype(jnp.float32)
    all_rows, all_tags = side_by_side((shade_rows, tagged), "gauss", 0, 1)
    own_tags = jnp.where(alive_mask, pix_ids + 1, -1).astype(jnp.float32)
    match_hot = (own_tags[:, None] == all_tags[None, :]).astype(jnp.float32)
    jp_rows = jnp.dot(match_hot, all_rows, precision=lax.Precision.HIGHEST)
    jp_round = jp_rows.astype(jnp.bfloat16)
    curv_terms = jnp.einsum("tpgx,tx->tpg", tiles_now, jp_round, preferred_element_type=jnp.float32)
    curv_acc = jnp.sum(block_hot.T[:, :, None, None] * curv_terms[None], axis=1)
    resid_rows = jnp.take(residual[0], pix_ids, axis=0)
    grad_terms = jnp.einsum(
        "tpgx,tx->tpg", tiles_now, resid_rows, preferred_element_type=jnp.float32
    )
    grad_acc = jnp.sum(block_hot.T[:, :, None, None] * grad_terms[None], axis=1)
    both_sum = over_copies(jnp.stack([grad_acc, curv_acc]), "view")
    return (both_sum[0], both_sum[1], gram_sum)


def solution(mesh):
    placed = (
        P("view", "gauss", None, None, None),
        P("view", "gauss"),
        P("view", "gauss"),
        P("view", "gauss"),
        P("view", None, None),
        P("gauss", None, None),
    )
    return jax.shard_map(
        local,
        mesh=mesh,
        in_specs=placed,
        out_specs=(P("gauss", None, None), P("gauss", None, None), P("gauss", None, None, None)),
        check_vma=False,
    )
```

```python
import math

import jax
import jax.numpy as jnp
import numpy as np
from jax import lax
from jax.sharding import PartitionSpec as P
from jax.experimental import pallas as pl
from jax.experimental.pallas import tpu as pltpu


def side_by_side(arrays, axis, dim, along):
    widths = [math.prod(a.shape[along:]) for a in arrays]
    both = jnp.concatenate(
        [a.reshape(*a.shape[:along], w) for a, w in zip(arrays, widths)], axis=along
    )
    result = copy_for_each(both, axis).reshape(-1, *both.shape[1:])
    blocks = jnp.split(result, [sum(widths[:k]) for k in range(1, len(widths))], axis=along)
    return tuple(
        (b.reshape(*result.shape[:along], *a.shape[along:]) for a, b in zip(arrays, blocks))
    )


def copy_for_each(array, axis):
    length = lax.axis_size(axis)
    return lax.all_to_all(
        jnp.broadcast_to(array[None], (length, *array.shape)), axis, 0, 0, tiled=True
    )


def over_copies(array, axis):
    everything = copy_for_each(array, axis)
    return jnp.sum(everything, axis=0)


P_PAD = 64
GROUP = 2


def row_offsets(size):
    return [p * size - p * (p - 1) // 2 for p in range(size)]


def gram_kernel(w_ref, jac_ref, out_ref, xf_ref, sc_ref, acc_ref):
    t = pl.program_id(0)
    size = jac_ref.shape[0]
    gb = jac_ref.shape[1]
    nb = acc_ref.shape[0]
    halves = xf_ref.shape[0]
    span = P_PAD * 8

    @pl.when(t == 0)
    def _init():
        for h in range(halves):
            for c in range(gb // 8):
                xf_ref[h, pl.ds(c * span + size * 8, (P_PAD - size) * 8), :] = jnp.zeros(((P_PAD - size) * 8, 128), jnp.float32)
        acc_ref[...] = jnp.zeros(acc_ref.shape, jnp.float32)

    for p in range(size):
        for h in range(halves):
            slab = jac_ref[p, :, h * 128:(h + 1) * 128].astype(jnp.float32)
            for c in range(gb // 8):
                xf_ref[h, pl.ds(c * span + p * 8, 8), :] = slab[c * 8:(c + 1) * 8]

    for c in range(gb // GROUP):
        parts = []
        for i in range(GROUP):
            g = c * GROUP + i
            base = (g // 8) * span + g % 8
            parts.append(jnp.concatenate([xf_ref[h, pl.ds(base, P_PAD, stride=8), :] for h in range(halves)], axis=1))
        a = jnp.concatenate(parts, axis=0).astype(jnp.bfloat16)
        prod = lax.dot_general(a, a, (((1,), (1,)), ((), ())), preferred_element_type=jnp.float32)
        for i in range(GROUP):
            g = c * GROUP + i
            lane0 = 128 * ((i * P_PAD) // 128)
            block = prod[i * P_PAD:(i + 1) * P_PAD, lane0:lane0 + 128]
            for r in range(P_PAD // 8):
                sc_ref[pl.ds(r * gb * 8 + g * 8, 8), :] = block[r * 8:(r + 1) * 8]

    odd = (lax.broadcasted_iota(jnp.int32, (P_PAD, gb), 1) % 2) == 1
    alive = w_ref[t, 0]
    blk = jnp.int32(0)
    for b in range(1, nb):
        alive = alive + w_ref[t, b]
        blk = jnp.where(w_ref[t, b] > 0, jnp.int32(b), blk)
    for p in range(size):
        s = sc_ref[pl.ds((p // 8) * gb * 8 + p % 8, gb, stride=8), :]
        tr = s.T
        row = jnp.where(odd, tr[P_PAD:2 * P_PAD], tr[0:P_PAD])
        acc_ref[blk, p] += alive * row

    @pl.when(t == pl.num_programs(0) - 1)
    def _pack():
        offs = row_offsets(size)
        for b in range(nb):
            for p in range(size):
                out_ref[b, pl.ds(offs[p], size - p), :] = acc_ref[b, p, pl.ds(p, size - p), :]


def gram_packed(tiles, weights):
    nt, size, gb, nx = tiles.shape
    nb = weights.shape[1]
    packed_rows = size * (size + 1) // 2
    return pl.pallas_call(
        gram_kernel,
        grid=(nt,),
        in_specs=[
            pl.BlockSpec(memory_space=pltpu.SMEM),
            pl.BlockSpec((None, size, gb, nx), lambda t: (t, 0, 0, 0)),
        ],
        out_specs=pl.BlockSpec((nb, packed_rows, gb), lambda t: (0, 0, 0)),
        out_shape=jax.ShapeDtypeStruct((nb, packed_rows, gb), jnp.float32),
        scratch_shapes=[
            pltpu.VMEM((nx // 128, P_PAD * gb, 128), jnp.float32),
            pltpu.VMEM((gb * P_PAD, 128), jnp.float32),
            pltpu.VMEM((nb, size, P_PAD, gb), jnp.float32),
        ],
        compiler_params=pltpu.CompilerParams(vmem_limit_bytes=48 * 1024 * 1024),
    )(weights, tiles)


ROW_CHUNK = 16


def unpack_kernel(packed_ref, out_ref, u_ref):
    step = pl.program_id(0)
    size, nb = out_ref.shape[1], out_ref.shape[2]
    offs = row_offsets(size)
    span = P_PAD * 8
    q_id = lax.broadcasted_iota(jnp.int32, (P_PAD, out_ref.shape[3]), 0)

    @pl.when(step == 0)
    def _fill():
        for b in range(nb):
            for p in range(size):
                for qb in range(p // 8, pl.cdiv(size, 8)):
                    q0 = max(p, qb * 8)
                    q1 = min(size, qb * 8 + 8)
                    u_ref[b, pl.ds(qb * span + p * 8 + q0 % 8, q1 - q0), :] = packed_ref[b, pl.ds(offs[p] + q0 - p, q1 - q0), :]

    for c in range(pl.cdiv(size, ROW_CHUNK)):
        @pl.when(step == c)
        def _rows():
            for p in range(c * ROW_CHUNK, min(size, (c + 1) * ROW_CHUNK)):
                rows = []
                for b in range(nb):
                    up = jnp.concatenate([u_ref[b, pl.ds(qb * span + p * 8, 8), :] for qb in range(P_PAD // 8)], axis=0)
                    low = u_ref[b, pl.ds((p // 8) * span + p % 8, P_PAD, stride=8), :]
                    rows.append(jnp.where(q_id >= p, up, low)[0:size])
                out_ref[p - c * ROW_CHUNK] = jnp.stack(rows, axis=1)


def unpack(packed, size):
    nb, rows, gb = packed.shape
    full = pl.pallas_call(
        unpack_kernel,
        grid=(pl.cdiv(size, ROW_CHUNK),),
        in_specs=[pl.BlockSpec((nb, rows, gb), lambda i: (0, 0, 0))],
        out_specs=pl.BlockSpec((ROW_CHUNK, size, nb, gb), lambda i: (i, 0, 0, 0)),
        out_shape=jax.ShapeDtypeStruct((size, size, nb, gb), jnp.float32),
        scratch_shapes=[pltpu.VMEM((nb, P_PAD * P_PAD, gb), jnp.float32)],
    )(packed)
    return jnp.transpose(full, (2, 0, 1, 3))


def local(jac, tile_count, tile_block, tile_pix, residual, direction):
    slot_total = jac.shape[1]
    blocks = direction.shape[0]
    size = jac.shape[2]
    live_count = tile_count[0, 0]
    block_ids = tile_block[0]
    pix_ids = tile_pix[0]
    alive_mask = jnp.arange(slot_total) < live_count
    alive_float = alive_mask.astype(jnp.float32)
    tiles_now = jac[0]
    block_match = block_ids[:, None] == jnp.arange(blocks)[None, :]
    block_hot = (block_match & alive_mask[:, None]).astype(jnp.float32)

    packed_gram = gram_packed(tiles_now, block_hot)
    packed_gram, tiles_now = lax.optimization_barrier((packed_gram, tiles_now))
    summed = lax.psum(packed_gram, "view")
    gram_sum = unpack(summed, size)

    dir_rows = jnp.take(direction, block_ids, axis=0)
    shade_rows = (
        jnp.einsum("tpgx,tpg->tx", tiles_now, dir_rows, preferred_element_type=jnp.float32)
        * alive_float[:, None]
    )
    tagged = jnp.where(alive_mask, pix_ids + 1, 0).astype(jnp.float32)
    all_rows, all_tags = side_by_side((shade_rows, tagged), "gauss", 0, 1)
    own_tags = jnp.where(alive_mask, pix_ids + 1, -1).astype(jnp.float32)
    match_hot = (own_tags[:, None] == all_tags[None, :]).astype(jnp.float32)
    jp_rows = jnp.dot(match_hot, all_rows, precision=lax.Precision.HIGHEST)
    jp_round = jp_rows.astype(jnp.bfloat16)
    curv_terms = jnp.einsum("tpgx,tx->tpg", tiles_now, jp_round, preferred_element_type=jnp.float32)
    curv_acc = jnp.sum(block_hot.T[:, :, None, None] * curv_terms[None], axis=1)
    resid_rows = jnp.take(residual[0], pix_ids, axis=0)
    grad_terms = jnp.einsum(
        "tpgx,tx->tpg", tiles_now, resid_rows, preferred_element_type=jnp.float32
    )
    grad_acc = jnp.sum(block_hot.T[:, :, None, None] * grad_terms[None], axis=1)
    both_sum = over_copies(jnp.stack([grad_acc, curv_acc]), "view")
    return (both_sum[0], both_sum[1], gram_sum)


def solution(mesh):
    placed = (
        P("view", "gauss", None, None, None),
        P("view", "gauss"),
        P("view", "gauss"),
        P("view", "gauss"),
        P("view", None, None),
        P("gauss", None, None),
    )
    return jax.shard_map(
        local,
        mesh=mesh,
        in_specs=placed,
        out_specs=(P("gauss", None, None), P("gauss", None, None), P("gauss", None, None, None)),
        check_vma=False,
    )
```

```python
import math

import jax
import jax.numpy as jnp
import numpy as np
from jax import lax
from jax.sharding import PartitionSpec as P
from jax.experimental import pallas as pl
from jax.experimental.pallas import tpu as pltpu


def side_by_side(arrays, axis, dim, along):
    widths = [math.prod(a.shape[along:]) for a in arrays]
    both = jnp.concatenate(
        [a.reshape(*a.shape[:along], w) for a, w in zip(arrays, widths)], axis=along
    )
    result = copy_for_each(both, axis).reshape(-1, *both.shape[1:])
    blocks = jnp.split(result, [sum(widths[:k]) for k in range(1, len(widths))], axis=along)
    return tuple(
        (b.reshape(*result.shape[:along], *a.shape[along:]) for a, b in zip(arrays, blocks))
    )


def copy_for_each(array, axis):
    length = lax.axis_size(axis)
    return lax.all_to_all(
        jnp.broadcast_to(array[None], (length, *array.shape)), axis, 0, 0, tiled=True
    )


def over_copies(array, axis):
    everything = copy_for_each(array, axis)
    return jnp.sum(everything, axis=0)


P_PAD = 64
GROUP = 2


def row_offsets(size):
    return [p * size - p * (p - 1) // 2 for p in range(size)]


def gram_kernel(w_ref, jac_ref, out_ref, xf_ref, sc_ref, acc_ref):
    t = pl.program_id(0)
    size = jac_ref.shape[0]
    gb = jac_ref.shape[1]
    nb = acc_ref.shape[0]
    halves = xf_ref.shape[0]
    span = P_PAD * 8

    @pl.when(t == 0)
    def _init():
        for h in range(halves):
            for c in range(gb // 8):
                xf_ref[h, pl.ds(c * span + size * 8, (P_PAD - size) * 8), :] = jnp.zeros(((P_PAD - size) * 8, 128), jnp.float32)
        acc_ref[...] = jnp.zeros(acc_ref.shape, jnp.float32)

    for p in range(size):
        for h in range(halves):
            slab = jac_ref[p, :, h * 128:(h + 1) * 128].astype(jnp.float32)
            for c in range(gb // 8):
                xf_ref[h, pl.ds(c * span + p * 8, 8), :] = slab[c * 8:(c + 1) * 8]

    for c in range(gb // GROUP):
        parts = []
        for i in range(GROUP):
            g = c * GROUP + i
            base = (g // 8) * span + g % 8
            parts.append(jnp.concatenate([xf_ref[h, pl.ds(base, P_PAD, stride=8), :] for h in range(halves)], axis=1))
        a = jnp.concatenate(parts, axis=0).astype(jnp.bfloat16)
        prod = lax.dot_general(a, a, (((1,), (1,)), ((), ())), preferred_element_type=jnp.float32)
        for i in range(GROUP):
            g = c * GROUP + i
            lane0 = 128 * ((i * P_PAD) // 128)
            block = prod[i * P_PAD:(i + 1) * P_PAD, lane0:lane0 + 128]
            for r in range(P_PAD // 8):
                sc_ref[pl.ds(r * gb * 8 + g * 8, 8), :] = block[r * 8:(r + 1) * 8]

    odd = (lax.broadcasted_iota(jnp.int32, (P_PAD, gb), 1) % 2) == 1
    alive = w_ref[t, 0]
    blk = jnp.int32(0)
    for b in range(1, nb):
        alive = alive + w_ref[t, b]
        blk = jnp.where(w_ref[t, b] > 0, jnp.int32(b), blk)
    for p in range(size):
        s = sc_ref[pl.ds((p // 8) * gb * 8 + p % 8, gb, stride=8), :]
        tr = s.T
        row = jnp.where(odd, tr[P_PAD:2 * P_PAD], tr[0:P_PAD])
        acc_ref[blk, p] += alive * row

    @pl.when(t == pl.num_programs(0) - 1)
    def _pack():
        offs = row_offsets(size)
        for b in range(nb):
            for p in range(size):
                out_ref[b, pl.ds(offs[p], size - p), :] = acc_ref[b, p, pl.ds(p, size - p), :]


def gram_packed(tiles, weights):
    nt, size, gb, nx = tiles.shape
    nb = weights.shape[1]
    packed_rows = size * (size + 1) // 2
    return pl.pallas_call(
        gram_kernel,
        grid=(nt,),
        in_specs=[
            pl.BlockSpec(memory_space=pltpu.SMEM),
            pl.BlockSpec((None, size, gb, nx), lambda t: (t, 0, 0, 0)),
        ],
        out_specs=pl.BlockSpec((nb, packed_rows, gb), lambda t: (0, 0, 0)),
        out_shape=jax.ShapeDtypeStruct((nb, packed_rows, gb), jnp.float32),
        scratch_shapes=[
            pltpu.VMEM((nx // 128, P_PAD * gb, 128), jnp.float32),
            pltpu.VMEM((gb * P_PAD, 128), jnp.float32),
            pltpu.VMEM((nb, size, P_PAD, gb), jnp.float32),
        ],
        compiler_params=pltpu.CompilerParams(vmem_limit_bytes=48 * 1024 * 1024),
    )(weights, tiles)


ROW_CHUNK = 32


def unpack_kernel(packed_ref, out_ref, u_ref):
    step = pl.program_id(0)
    size, nb = out_ref.shape[1], out_ref.shape[2]
    offs = row_offsets(size)
    span = P_PAD * 8
    q_id = lax.broadcasted_iota(jnp.int32, (P_PAD, out_ref.shape[3]), 0)

    @pl.when(step == 0)
    def _fill():
        for b in range(nb):
            for p in range(size):
                for qb in range(p // 8, pl.cdiv(size, 8)):
                    q0 = max(p, qb * 8)
                    q1 = min(size, qb * 8 + 8)
                    u_ref[b, pl.ds(qb * span + p * 8 + q0 % 8, q1 - q0), :] = packed_ref[b, pl.ds(offs[p] + q0 - p, q1 - q0), :]

    for c in range(pl.cdiv(size, ROW_CHUNK)):
        @pl.when(step == c)
        def _rows():
            for p in range(c * ROW_CHUNK, min(size, (c + 1) * ROW_CHUNK)):
                rows = []
                for b in range(nb):
                    up = jnp.concatenate([u_ref[b, pl.ds(qb * span + p * 8, 8), :] for qb in range(P_PAD // 8)], axis=0)
                    low = u_ref[b, pl.ds((p // 8) * span + p % 8, P_PAD, stride=8), :]
                    rows.append(jnp.where(q_id >= p, up, low)[0:size])
                out_ref[p - c * ROW_CHUNK] = jnp.stack(rows, axis=1)


def unpack(packed, size):
    nb, rows, gb = packed.shape
    full = pl.pallas_call(
        unpack_kernel,
        grid=(pl.cdiv(size, ROW_CHUNK),),
        in_specs=[pl.BlockSpec((nb, rows, gb), lambda i: (0, 0, 0))],
        out_specs=pl.BlockSpec((ROW_CHUNK, size, nb, gb), lambda i: (i, 0, 0, 0)),
        out_shape=jax.ShapeDtypeStruct((size, size, nb, gb), jnp.float32),
        scratch_shapes=[pltpu.VMEM((nb, P_PAD * P_PAD, gb), jnp.float32)],
    )(packed)
    return jnp.transpose(full, (2, 0, 1, 3))


def local(jac, tile_count, tile_block, tile_pix, residual, direction):
    slot_total = jac.shape[1]
    blocks = direction.shape[0]
    size = jac.shape[2]
    live_count = tile_count[0, 0]
    block_ids = tile_block[0]
    pix_ids = tile_pix[0]
    alive_mask = jnp.arange(slot_total) < live_count
    alive_float = alive_mask.astype(jnp.float32)
    tiles_now = jac[0]
    block_match = block_ids[:, None] == jnp.arange(blocks)[None, :]
    block_hot = (block_match & alive_mask[:, None]).astype(jnp.float32)

    packed_gram = gram_packed(tiles_now, block_hot)
    packed_gram, tiles_now = lax.optimization_barrier((packed_gram, tiles_now))
    summed = lax.psum(packed_gram, "view")
    gram_sum = unpack(summed, size)

    dir_rows = jnp.take(direction, block_ids, axis=0)
    shade_rows = (
        jnp.einsum("tpgx,tpg->tx", tiles_now, dir_rows, preferred_element_type=jnp.float32)
        * alive_float[:, None]
    )
    tagged = jnp.where(alive_mask, pix_ids + 1, 0).astype(jnp.float32)
    all_rows, all_tags = side_by_side((shade_rows, tagged), "gauss", 0, 1)
    own_tags = jnp.where(alive_mask, pix_ids + 1, -1).astype(jnp.float32)
    match_hot = (own_tags[:, None] == all_tags[None, :]).astype(jnp.float32)
    jp_rows = jnp.dot(match_hot, all_rows, precision=lax.Precision.HIGHEST)
    jp_round = jp_rows.astype(jnp.bfloat16)
    curv_terms = jnp.einsum("tpgx,tx->tpg", tiles_now, jp_round, preferred_element_type=jnp.float32)
    curv_acc = jnp.sum(block_hot.T[:, :, None, None] * curv_terms[None], axis=1)
    resid_rows = jnp.take(residual[0], pix_ids, axis=0)
    grad_terms = jnp.einsum(
        "tpgx,tx->tpg", tiles_now, resid_rows, preferred_element_type=jnp.float32
    )
    grad_acc = jnp.sum(block_hot.T[:, :, None, None] * grad_terms[None], axis=1)
    both_sum = over_copies(jnp.stack([grad_acc, curv_acc]), "view")
    return (both_sum[0], both_sum[1], gram_sum)


def solution(mesh):
    placed = (
        P("view", "gauss", None, None, None),
        P("view", "gauss"),
        P("view", "gauss"),
        P("view", "gauss"),
        P("view", None, None),
        P("gauss", None, None),
    )
    return jax.shard_map(
        local,
        mesh=mesh,
        in_specs=placed,
        out_specs=(P("gauss", None, None), P("gauss", None, None), P("gauss", None, None, None)),
        check_vma=False,
    )
```
